512 devices in a mesh: tm: 16 (over z_lo, core), fsdp: 32 (over x, y, z_hi).
Axes of the slice: x: 4, y: 4, z: 16 (z_hi: 2, z_lo: 8; z = z_hi * 8 + z_lo), core: 2. Of those that a mesh axis runs over, the one named last changes fastest.
Arguments:
- frames: bfloat16 [32, 8192, 512], P('fsdp', 'tm'), may hold values from -12 to 12
- retention: float32 [32, 8192, 512], P('fsdp', 'tm'), may hold values from 0.4 to 1
- first_conv: bfloat16 [1024, 1024], P('fsdp'), may hold values from -0.1875 to 0.1875
- second_conv: bfloat16 [1024, 1024], P('fsdp'), may hold values from -0.1875 to 0.1875
- cotangent: bfloat16 [32, 8192, 512], P('fsdp', 'tm'), may hold values from -0.03125 to 0.03125
Outputs:
- top_hidden: bfloat16 [32, 8192, 512], P('fsdp', 'tm')
- grad_first: float32 [1024, 1024], P('fsdp')
- grad_second: float32 [1024, 1024], P('fsdp')
The draws below stay inside these ranges and needn't reach their ends.
All inputs are finite; a program needn't handle non-finite values.
Results may differ from the reference program's by a relative error of at most 0.035.
Values may be sent and summed in bfloat16 or wider, within the bound.
No kernel may reach another device: no remote copies, remote signals or barrier semaphores. Data moves between devices by JAX's collectives and lax.ppermute only.
A program may use at most 128 MiB of HBM per device.

```python
import math
import jax
import jax.numpy as jnp
from jax import lax

RESIDUAL_WIDTH = 512
FRAMES_DEV = 512
SHORT_SPACING = 128
LONG_SPACING = 512
TRACE_DURATION = 8192
TRACE_TOTAL = 32


def draw_frames(key, part):
    stochastic_seeds = jax.random.split(jax.random.fold_in(key, 11), 3)
    levels = 1.5 * jax.random.normal(stochastic_seeds[0], (TRACE_TOTAL, 1, RESIDUAL_WIDTH), jnp.float32)
    jitter = jax.random.normal(stochastic_seeds[1], (TRACE_TOTAL, TRACE_DURATION, RESIDUAL_WIDTH), jnp.float32)
    pairing = jax.random.permutation(stochastic_seeds[2], TRACE_TOTAL)
    owner_block = jnp.arange(RESIDUAL_WIDTH) * TRACE_TOTAL // RESIDUAL_WIDTH
    spike_gain = jnp.where(owner_block[None, :] == pairing[:, None], 3.0, 1.0)[:, None, :]
    payload_elements = (levels + jitter) * spike_gain
    return jnp.clip(payload_elements, -12.0, 12.0).astype(jnp.bfloat16)


def draw_retention(key, part):
    stochastic_seeds = jax.random.split(jax.random.fold_in(key, 23), 6)
    quick_share = 0.5
    fast_selector = jax.random.bernoulli(stochastic_seeds[0], quick_share, (TRACE_TOTAL, 1, RESIDUAL_WIDTH))
    fast_frequencies = jnp.exp(jax.random.uniform(stochastic_seeds[1], (TRACE_TOTAL, 1, RESIDUAL_WIDTH), jnp.float32, math.log(1.0 / 50.0), math.log(1.0 / 30.0)))
    gradual_frequencies = jax.random.uniform(stochastic_seeds[2], (TRACE_TOTAL, 1, RESIDUAL_WIDTH), jnp.float32, 0.15, 0.5) / TRACE_DURATION
    spike_frequencies = jnp.where(fast_selector, fast_frequencies, gradual_frequencies)
    group_scale = jnp.exp(jax.random.uniform(stochastic_seeds[3], (TRACE_TOTAL, TRACE_DURATION // FRAMES_DEV, 1), jnp.float32, math.log(0.5), math.log(2.0)))
    group_scale = jnp.repeat(group_scale, FRAMES_DEV, axis=1)
    spell_locus = jax.random.randint(stochastic_seeds[4], (TRACE_TOTAL, 1, 3), 0, TRACE_DURATION)
    timestep_number = jnp.arange(TRACE_DURATION)[None, :, None]
    spell_on = jnp.any(timestep_number == spell_locus, axis=2)[:, :, None]
    spell_persistence = jax.random.uniform(stochastic_seeds[5], (TRACE_TOTAL, TRACE_DURATION, 1), jnp.float32, 0.5, 0.8)
    payload_elements = jnp.exp(-spike_frequencies * group_scale) * jnp.where(spell_on, spell_persistence, 1.0)
    return payload_elements.astype(jnp.float32)


def level_of(key, shape, shards, least, largest):
    def one(dim, blocks):
        steps = jax.random.uniform(jax.random.fold_in(jax.random.fold_in(key, 6), dim), (blocks,), jnp.float32, least / len(shards), largest / len(shards))
        return jnp.repeat(jnp.exp(steps), shape[dim] // blocks).reshape((-1,) + (1,) * (len(shape) - dim - 1))

    factor_of = one(*shards[0])
    for cut in shards[1:]:
        factor_of = factor_of * one(*cut)
    return factor_of


def scatter_about(stream_key, dims, deviation, most, cuts=(), held_as=jnp.bfloat16):
    array = deviation * jax.random.normal(stream_key, dims, jnp.float32)
    if cuts:
        array = array * level_of(stream_key, dims, cuts, -0.22, 0.18)
    return jnp.clip(array, -most, most).astype(held_as)


def setup_inputs(seed: int = 0) -> dict:
    seeds = jax.random.split(jax.random.key(seed), 6)
    return {
        "frames": draw_frames(jax.random.fold_in(seeds[5], 71), 0),
        "retention": draw_retention(jax.random.fold_in(seeds[5], 71), 0),
        "first_conv": scatter_about(seeds[2], (2 * RESIDUAL_WIDTH, 2 * RESIDUAL_WIDTH), (2 * RESIDUAL_WIDTH) ** -0.5, 0.1875, ((0, 32),)),
        "second_conv": scatter_about(seeds[3], (2 * RESIDUAL_WIDTH, 2 * RESIDUAL_WIDTH), (2 * RESIDUAL_WIDTH) ** -0.5, 0.1875, ((0, 32),)),
        "cotangent": scatter_about(seeds[4], (TRACE_TOTAL, TRACE_DURATION, RESIDUAL_WIDTH), ((TRACE_TOTAL * TRACE_DURATION) ** -0.5), 0.03125, ((0, 32), (1, 16))),
    }


def combine_maps(earlier, later):
    return (earlier[0] * later[0], later[0] * earlier[1] + later[1])

def gated(pre_values):
    split_at = pre_values.shape[1] // 2
    return jnp.tanh(pre_values[:, :split_at]) * jax.nn.sigmoid(pre_values[:, split_at:])

def gate_grad(pre_values, incoming_gradient):
    split_at = pre_values.shape[1] // 2
    tanh_part = jnp.tanh(pre_values[:, :split_at])
    gate_part = jax.nn.sigmoid(pre_values[:, split_at:])
    return jnp.concatenate([incoming_gradient * gate_part * (1.0 - tanh_part * tanh_part), incoming_gradient * tanh_part * gate_part * (1.0 - gate_part)], axis=1)

def lagged_input(payload_elements, shift_by):
    return jnp.concatenate([jnp.zeros((shift_by, payload_elements.shape[1]), payload_elements.dtype), payload_elements[:payload_elements.shape[0] - shift_by]], axis=0)

def shifted_ahead(payload_elements, shift_by):
    return jnp.concatenate([payload_elements[shift_by:], jnp.zeros((shift_by, payload_elements.shape[1]), payload_elements.dtype)], axis=0)

def block_sums(operand, gradients):
    blocks = operand.shape[0] // FRAMES_DEV
    left_side = operand.reshape(blocks, FRAMES_DEV, operand.shape[1]).astype(jnp.float32)
    right_side = gradients.reshape(blocks, FRAMES_DEV, gradients.shape[1]).astype(jnp.float32)
    partials = jnp.einsum('kti,ktj->kij', left_side, right_side)
    rounded = lax.optimization_barrier(partials.astype(jnp.bfloat16))
    return lax.optimization_barrier(jnp.sum(rounded.astype(jnp.float32), axis=0))

def reference(frames, retention, first_conv, second_conv, cotangent):

    def one_sequence(totals, inputs):
        sequence, keep_rate, upstream_in = inputs
        payload_elements = sequence.astype(jnp.float32)
        factor, baseline = lax.associative_scan(combine_maps, (keep_rate, (1.0 - keep_rate) * payload_elements), axis=0)
        trend_removed = (payload_elements - baseline).astype(jnp.bfloat16)
        opening_layer_input = jnp.concatenate([lagged_input(trend_removed, SHORT_SPACING), trend_removed], axis=1)
        first_pre = jnp.dot(opening_layer_input, first_conv, preferred_element_type=jnp.float32)
        opening_layer_output = (trend_removed.astype(jnp.float32) + gated(first_pre)).astype(jnp.bfloat16)
        closing_layer_input = jnp.concatenate([lagged_input(opening_layer_output, LONG_SPACING), opening_layer_output], axis=1)
        second_pre = jnp.dot(closing_layer_input, second_conv, preferred_element_type=jnp.float32)
        top_hidden = (opening_layer_output.astype(jnp.float32) + gated(second_pre)).astype(jnp.bfloat16)
        incoming_gradient = upstream_in.astype(jnp.float32)
        second_grad = gate_grad(second_pre, incoming_gradient).astype(jnp.bfloat16)
        closing_backward = jnp.dot(second_grad, second_conv.T, preferred_element_type=jnp.float32)
        opening_upstream_gradient = incoming_gradient + closing_backward[:, RESIDUAL_WIDTH:] + shifted_ahead(closing_backward[:, :RESIDUAL_WIDTH], LONG_SPACING)
        first_grad = gate_grad(first_pre, opening_upstream_gradient).astype(jnp.bfloat16)
        new_totals = (totals[0] + block_sums(opening_layer_input, first_grad), totals[1] + block_sums(closing_layer_input, second_grad))
        return (new_totals, top_hidden)
    empty = jnp.zeros((2 * RESIDUAL_WIDTH, 2 * RESIDUAL_WIDTH), jnp.float32)
    totals, top_hidden = lax.scan(one_sequence, (empty, empty), (frames, retention, cotangent))
    return (top_hidden, totals[0], totals[1])
```

```python
import jax
import jax.numpy as jnp
from jax import lax
from jax.sharding import Mesh, PartitionSpec as P


def passed_along(value, axis, steps):
    count = 16
    leading, last = (max(0, -steps), min(count, count - steps))
    return lax.ppermute(value, axis, [(source, source + steps) for source in range(leading, last)])


TM = ("zl", "c")
SUB_AXES = ("zl", "c", "x", "y", "zh")


def rotated(value, axis, size, steps):
    return lax.ppermute(value, axis, [(i, (i + steps) % size) for i in range(size)])


def gather_over(block, axis, size, dim):
    place = lax.axis_index(axis)
    width = block.shape[dim]
    shape = list(block.shape)
    shape[dim] = width * size
    out = lax.dynamic_update_slice_in_dim(jnp.zeros(shape, block.dtype), block, place * width, dim)
    for steps in range(1, size):
        arrived = rotated(block, axis, size, steps)
        out = lax.dynamic_update_slice_in_dim(out, arrived, ((place - steps) % size) * width, dim)
    return out


def scatter_over(total, axis, size, dim):
    place = lax.axis_index(axis)
    width = total.shape[dim] // size
    sent = total.astype(jnp.bfloat16)
    acc = lax.dynamic_slice_in_dim(total, place * width, width, dim).astype(jnp.float32)
    for steps in range(1, size):
        piece = lax.dynamic_slice_in_dim(sent, ((place + steps) % size) * width, width, dim)
        acc = acc + rotated(piece, axis, size, steps).astype(jnp.float32)
    return acc


def summed_over(total, axis, size):
    stride = 1
    while stride < size:
        partner = lax.ppermute(total, axis, [(i, i ^ stride) for i in range(size)])
        total = total + partner
        stride *= 2
    return total


def gather_weight(shard):
    core = lax.axis_index("c")
    half = shard.shape[1] // 2
    mine = lax.dynamic_slice_in_dim(shard, core * half, half, 1)
    rows = gather_over(gather_over(gather_over(mine, "zh", 2, 0), "y", 4, 0), "x", 4, 0)
    return gather_over(rows, "c", 2, 1)


def reduce_gradient(partial):
    partial = partial.astype(jnp.bfloat16)
    cols = scatter_over(partial, "c", 2, 1)
    rows = scatter_over(scatter_over(scatter_over(cols, "x", 4, 0), "y", 4, 0), "zh", 2, 0)
    total = summed_over(rows, "zl", 8)
    return gather_over(total, "c", 2, 1)


def prefix_state(state, size):
    place = lax.axis_index(TM)
    stride = 1
    while stride < size:
        earlier = passed_along(state, TM, stride)
        joined = jnp.stack(combine_maps((earlier[0], earlier[1]), (state[0], state[1])))
        state = jnp.where(place >= stride, joined, state)
        stride *= 2
    return state


def combine_maps(earlier, later):
    return (earlier[0] * later[0], later[0] * earlier[1] + later[1])


def gated(pre_values):
    split_at = pre_values.shape[1] // 2
    return jnp.tanh(pre_values[:, :split_at]) * jax.nn.sigmoid(pre_values[:, split_at:])


def gate_grad(pre_values, incoming_gradient):
    split_at = pre_values.shape[1] // 2
    tanh_part = jnp.tanh(pre_values[:, :split_at])
    gate_part = jax.nn.sigmoid(pre_values[:, split_at:])
    return jnp.concatenate(
        [
            incoming_gradient * gate_part * (1.0 - tanh_part * tanh_part),
            incoming_gradient * tanh_part * gate_part * (1.0 - gate_part),
        ],
        axis=1,
    )


def accumulate_with(operand, weights_block):
    return jnp.dot(operand, weights_block, preferred_element_type=jnp.float32)


def back_with(gradients, weights_block):
    return lax.dot_general(
        gradients, weights_block, (((1,), (1,)), ((), ())), preferred_element_type=jnp.float32
    )


def weight_term(operand, gradients):
    return lax.dot_general(
        operand, gradients, (((0,), (0,)), ((), ())), preferred_element_type=jnp.float32
    )


def on_device(frames, retention, first_conv, second_conv, cotangent):
    first_full = gather_weight(first_conv)
    second_full = gather_weight(second_conv)
    payload_elements = frames[0].astype(jnp.float32)
    keep_rate = retention[0]
    length, channels = payload_elements.shape
    short_lag = length // 4
    factor, local_part = lax.associative_scan(
        combine_maps, (keep_rate, (1.0 - keep_rate) * payload_elements), axis=0
    )
    through = prefix_state(jnp.stack([factor[-1], local_part[-1]]), 16)
    carried_level = passed_along(through[1], TM, 1)
    trend_removed = (payload_elements - (local_part + factor * carried_level[None, :])).astype(
        jnp.bfloat16
    )
    tail_rows = trend_removed[length - short_lag :]
    near_tail = passed_along(tail_rows, TM, 1)
    own_past = jnp.concatenate([near_tail, trend_removed[: length - short_lag]], axis=0)
    opening_layer_input = jnp.concatenate([own_past, trend_removed], axis=1)
    stacked_pre = accumulate_with(
        opening_layer_input, first_full
    )
    stacked_out = (trend_removed.astype(jnp.float32) + gated(stacked_pre)).astype(jnp.bfloat16)
    earlier_out = passed_along(stacked_out, TM, 1)
    closing_layer_input = jnp.concatenate([earlier_out, stacked_out], axis=1)
    second_pre = accumulate_with(
        closing_layer_input, second_full
    )
    top_hidden = (stacked_out.astype(jnp.float32) + gated(second_pre)).astype(jnp.bfloat16)
    incoming_gradient = cotangent[0].astype(jnp.float32)
    second_grad = gate_grad(second_pre, incoming_gradient).astype(jnp.bfloat16)
    grad_second = reduce_gradient(weight_term(closing_layer_input, second_grad))
    closing_backward = back_with(
        second_grad, second_full
    )
    carried_back = passed_along(
        closing_backward[:, :channels].astype(jnp.bfloat16), TM, -1
    ).astype(jnp.float32)
    opening_upstream_gradient = incoming_gradient + closing_backward[:, channels:] + carried_back
    first_grad = gate_grad(stacked_pre, opening_upstream_gradient).astype(jnp.bfloat16)
    grad_first = reduce_gradient(weight_term(opening_layer_input, first_grad))
    return (top_hidden[None], grad_first, grad_second)


def solution(mesh):
    tm, fsdp = mesh.shape["tm"], mesh.shape["fsdp"]
    split = mesh.devices.reshape(tm // 2, 2, 4, fsdp // 8, 2)
    sub = Mesh(split, SUB_AXES)
    rows, frames = ("x", "y", "zh"), TM
    in_specs = (
        P(rows, frames, None),
        P(rows, frames, None),
        P(rows, None),
        P(rows, None),
        P(rows, frames, None),
    )
    out_specs = (P(rows, frames, None), P(rows, None), P(rows, None))
    return jax.shard_map(
        on_device, mesh=sub, in_specs=in_specs, out_specs=out_specs, check_vma=False
    )
```

```python
import jax
import jax.numpy as jnp
from jax import lax
from jax.experimental import pallas as pl
from jax.sharding import Mesh, PartitionSpec as P


def passed_along(value, axis, steps):
    count = 16
    leading, last = (max(0, -steps), min(count, count - steps))
    return lax.ppermute(value, axis, [(source, source + steps) for source in range(leading, last)])


TM = ("zl", "c")
SUB_AXES = ("zl", "c", "x", "y", "zh")


def rotated(value, axis, size, steps):
    return lax.ppermute(value, axis, [(i, (i + steps) % size) for i in range(size)])


def gather_over(block, axis, size, dim):
    place = lax.axis_index(axis)
    width = block.shape[dim]
    shape = list(block.shape)
    shape[dim] = width * size
    out = lax.dynamic_update_slice_in_dim(jnp.zeros(shape, block.dtype), block, place * width, dim)
    for steps in range(1, size):
        arrived = rotated(block, axis, size, steps)
        out = lax.dynamic_update_slice_in_dim(out, arrived, ((place - steps) % size) * width, dim)
    return out


def scatter_over(total, axis, size, dim):
    place = lax.axis_index(axis)
    width = total.shape[dim] // size
    sent = total.astype(jnp.bfloat16)
    acc = lax.dynamic_slice_in_dim(total, place * width, width, dim).astype(jnp.float32)
    for steps in range(1, size):
        piece = lax.dynamic_slice_in_dim(sent, ((place + steps) % size) * width, width, dim)
        acc = acc + rotated(piece, axis, size, steps).astype(jnp.float32)
    return acc


def summed_over(total, axis, size):
    stride = 1
    while stride < size:
        partner = lax.ppermute(total, axis, [(i, i ^ stride) for i in range(size)])
        total = total + partner
        stride *= 2
    return total


def gather_weight(shard):
    core = lax.axis_index("c")
    half = shard.shape[2] // 2
    mine = lax.dynamic_slice_in_dim(shard, core * half, half, 2)
    rows = gather_over(gather_over(gather_over(mine, "zh", 2, 1), "y", 4, 1), "x", 4, 1)
    return gather_over(rows, "c", 2, 2)


def reduce_gradient(partial):
    partial = partial.astype(jnp.bfloat16)
    cols = scatter_over(partial, "c", 2, 2)
    rows = scatter_over(scatter_over(scatter_over(cols, "x", 4, 1), "y", 4, 1), "zh", 2, 1)
    total = summed_over(rows, "zl", 8)
    return gather_over(total, "c", 2, 2)


def prefix_state(state, size):
    place = lax.axis_index(TM)
    stride = 1
    while stride < size:
        earlier = passed_along(state, TM, stride)
        joined = jnp.stack(combine_maps((earlier[0], earlier[1]), (state[0], state[1])))
        state = jnp.where(place >= stride, joined, state)
        stride *= 2
    return state


def drift_body(emit, rate_ref, value_ref, start_ref, *out_refs):
    rows = rate_ref.shape[0]

    def block(b, level):
        base = pl.multiple_of(b * 8, 8)
        rate = rate_ref[pl.ds(base, 8), :]
        value = value_ref[pl.ds(base, 8), :]
        for i in range(8):
            keep = rate[i : i + 1, :]
            level = keep * level + (1.0 - keep) * value[i : i + 1, :]
            if emit:
                out_refs[0][pl.ds(base + i, 1), :] = value[i : i + 1, :] - level
        return level

    out_refs[-1][...] = lax.fori_loop(0, rows // 8, block, start_ref[...])


def drift(rate, value, start, emit):
    rows, channels = rate.shape
    outs = [jax.ShapeDtypeStruct((1, channels), jnp.float32)]
    if emit:
        outs = [jax.ShapeDtypeStruct((rows, channels), jnp.float32)] + outs
    return pl.pallas_call(lambda *refs: drift_body(emit, *refs), out_shape=outs)(rate, value, start)


def combine_maps(earlier, later):
    return (earlier[0] * later[0], later[0] * earlier[1] + later[1])


def gated(pre_values):
    split_at = pre_values.shape[1] // 2
    return jnp.tanh(pre_values[:, :split_at]) * jax.nn.sigmoid(pre_values[:, split_at:])


def gate_grad(pre_values, incoming_gradient):
    split_at = pre_values.shape[1] // 2
    tanh_part = jnp.tanh(pre_values[:, :split_at])
    gate_part = jax.nn.sigmoid(pre_values[:, split_at:])
    return jnp.concatenate(
        [
            incoming_gradient * gate_part * (1.0 - tanh_part * tanh_part),
            incoming_gradient * tanh_part * gate_part * (1.0 - gate_part),
        ],
        axis=1,
    )


def accumulate_with(operand, weights_block):
    return jnp.dot(operand, weights_block, preferred_element_type=jnp.float32)


def back_with(gradients, weights_block):
    return lax.dot_general(
        gradients, weights_block, (((1,), (1,)), ((), ())), preferred_element_type=jnp.float32
    )


def weight_term(operand, gradients):
    return lax.dot_general(
        operand, gradients, (((0,), (0,)), ((), ())), preferred_element_type=jnp.float32
    )


def on_device(frames, retention, first_conv, second_conv, cotangent):
    both_full = gather_weight(jnp.stack([first_conv, second_conv]))
    first_full, second_full = both_full[0], both_full[1]
    payload_elements = frames[0].astype(jnp.float32)
    keep_rate = retention[0]
    length, channels = payload_elements.shape
    short_lag = length // 4
    (local_last,) = drift(keep_rate, payload_elements, jnp.zeros((1, channels), jnp.float32), False)
    factor_last = jnp.prod(keep_rate, axis=0)
    through = prefix_state(jnp.stack([factor_last, local_last[0]]), 16)
    carried_level = passed_along(through[1], TM, 1)
    removed, _ = drift(keep_rate, payload_elements, carried_level[None, :], True)
    trend_removed = removed.astype(jnp.bfloat16)
    tail_rows = trend_removed[length - short_lag :]
    near_tail = passed_along(tail_rows, TM, 1)
    own_past = jnp.concatenate([near_tail, trend_removed[: length - short_lag]], axis=0)
    opening_layer_input = jnp.concatenate([own_past, trend_removed], axis=1)
    stacked_pre = accumulate_with(
        opening_layer_input, first_full
    )
    stacked_out = (trend_removed.astype(jnp.float32) + gated(stacked_pre)).astype(jnp.bfloat16)
    earlier_out = passed_along(stacked_out, TM, 1)
    closing_layer_input = jnp.concatenate([earlier_out, stacked_out], axis=1)
    second_pre = accumulate_with(
        closing_layer_input, second_full
    )
    top_hidden = (stacked_out.astype(jnp.float32) + gated(second_pre)).astype(jnp.bfloat16)
    incoming_gradient = cotangent[0].astype(jnp.float32)
    second_grad = gate_grad(second_pre, incoming_gradient).astype(jnp.bfloat16)
    second_term = weight_term(closing_layer_input, second_grad)
    closing_backward = back_with(
        second_grad, second_full
    )
    carried_back = passed_along(
        closing_backward[:, :channels].astype(jnp.bfloat16), TM, -1
    ).astype(jnp.float32)
    opening_upstream_gradient = incoming_gradient + closing_backward[:, channels:] + carried_back
    first_grad = gate_grad(stacked_pre, opening_upstream_gradient).astype(jnp.bfloat16)
    first_term = weight_term(opening_layer_input, first_grad)
    grads = reduce_gradient(jnp.stack([first_term, second_term]))
    grad_first, grad_second = grads[0], grads[1]
    return (top_hidden[None], grad_first, grad_second)


def solution(mesh):
    tm, fsdp = mesh.shape["tm"], mesh.shape["fsdp"]
    split = mesh.devices.reshape(tm // 2, 2, 4, fsdp // 8, 2)
    sub = Mesh(split, SUB_AXES)
    rows, frames = ("x", "y", "zh"), TM
    in_specs = (
        P(rows, frames, None),
        P(rows, frames, None),
        P(rows, None),
        P(rows, None),
        P(rows, frames, None),
    )
    out_specs = (P(rows, frames, None), P(rows, None), P(rows, None))
    return jax.shard_map(
        on_device, mesh=sub, in_specs=in_specs, out_specs=out_specs, check_vma=False
    )
```

```python
import jax
import jax.numpy as jnp
from jax import lax
from jax.experimental import pallas as pl
from jax.sharding import Mesh, PartitionSpec as P


def passed_along(value, axis, steps):
    count = 16
    leading, last = (max(0, -steps), min(count, count - steps))
    return lax.ppermute(value, axis, [(source, source + steps) for source in range(leading, last)])


TM = ("zl", "c")
SUB_AXES = ("zl", "c", "x", "y", "zh")


def rotated(value, axis, size, steps):
    return lax.ppermute(value, axis, [(i, (i + steps) % size) for i in range(size)])


def gather_over(block, axis, size, dim):
    place = lax.axis_index(axis)
    width = block.shape[dim]
    shape = list(block.shape)
    shape[dim] = width * size
    out = lax.dynamic_update_slice_in_dim(jnp.zeros(shape, block.dtype), block, place * width, dim)
    for steps in range(1, size):
        arrived = rotated(block, axis, size, steps)
        out = lax.dynamic_update_slice_in_dim(out, arrived, ((place - steps) % size) * width, dim)
    return out


def scatter_over(total, axis, size, dim):
    place = lax.axis_index(axis)
    width = total.shape[dim] // size
    sent = total.astype(jnp.bfloat16)
    acc = lax.dynamic_slice_in_dim(total, place * width, width, dim).astype(jnp.float32)
    for steps in range(1, size):
        piece = lax.dynamic_slice_in_dim(sent, ((place + steps) % size) * width, width, dim)
        acc = acc + rotated(piece, axis, size, steps).astype(jnp.float32)
    return acc


def summed_over(total, axis, size):
    stride = 1
    while stride < size:
        partner = lax.ppermute(total, axis, [(i, i ^ stride) for i in range(size)])
        total = total + partner
        stride *= 2
    return total


def drift_body(emit, rate_ref, value_ref, start_ref, *out_refs):
    rows = rate_ref.shape[0]

    def block(b, level):
        base = pl.multiple_of(b * 8, 8)
        rate = rate_ref[pl.ds(base, 8), :]
        value = value_ref[pl.ds(base, 8), :]
        for i in range(8):
            keep = rate[i : i + 1, :]
            level = keep * level + (1.0 - keep) * value[i : i + 1, :]
            if emit:
                out_refs[0][pl.ds(base + i, 1), :] = value[i : i + 1, :] - level
        return level

    out_refs[-1][...] = lax.fori_loop(0, rows // 8, block, start_ref[...])


def drift(rate, value, start, emit):
    rows, channels = rate.shape
    outs = [jax.ShapeDtypeStruct((1, channels), jnp.float32)]
    if emit:
        outs = [jax.ShapeDtypeStruct((rows, channels), jnp.float32)] + outs
    return pl.pallas_call(lambda *refs: drift_body(emit, *refs), out_shape=outs)(rate, value, start)


def spread_over(block, axis, count):
    copies = jnp.broadcast_to(block[None], (count,) + block.shape)
    return lax.all_to_all(copies, axis, 0, 0, tiled=True)


def gather_weights(shards):
    core = lax.axis_index("c")
    rows = gather_over(shards, "zh", 2, 1)
    half = rows.shape[2] // 2
    mine = lax.dynamic_slice_in_dim(rows, core * half, half, 2)
    got = spread_over(mine, ("c", "x", "y"), 32)
    count, block, width = mine.shape
    got = got.reshape(2, 16, count, block, width).transpose(2, 1, 3, 0, 4)
    return got.reshape(count, 16 * block, 2 * width)


def reduce_gradients(partials):
    count, height, width = partials.shape
    pieces = partials.astype(jnp.bfloat16).reshape(count, 16, height // 16, 2, width // 2)
    pieces = pieces.transpose(3, 1, 0, 2, 4).reshape(32, count, height // 16, width // 2)
    got = lax.all_to_all(pieces, ("c", "x", "y"), 0, 0, tiled=True)
    rows = scatter_over(jnp.sum(got.astype(jnp.float32), axis=0), "zh", 2, 1)
    total = summed_over(rows, "zl", 8)
    return gather_over(total, "c", 2, 2)


def carried_level(state, size):
    place = lax.axis_index(TM)
    every = spread_over(state, TM, size)
    level = jnp.ones_like(state[0]), jnp.zeros_like(state[1])
    for source in range(size - 1):
        joined = combine_maps(level, (every[source, 0], every[source, 1]))
        level = tuple(jnp.where(source < place, j, l) for j, l in zip(joined, level))
    return level[1]


def combine_maps(earlier, later):
    return (earlier[0] * later[0], later[0] * earlier[1] + later[1])


def gated(pre_values):
    split_at = pre_values.shape[1] // 2
    return jnp.tanh(pre_values[:, :split_at]) * jax.nn.sigmoid(pre_values[:, split_at:])


def gate_grad(pre_values, incoming_gradient):
    split_at = pre_values.shape[1] // 2
    tanh_part = jnp.tanh(pre_values[:, :split_at])
    gate_part = jax.nn.sigmoid(pre_values[:, split_at:])
    return jnp.concatenate(
        [
            incoming_gradient * gate_part * (1.0 - tanh_part * tanh_part),
            incoming_gradient * tanh_part * gate_part * (1.0 - gate_part),
        ],
        axis=1,
    )


def accumulate_with(operand, weights_block):
    return jnp.dot(operand, weights_block, preferred_element_type=jnp.float32)


def back_with(gradients, weights_block):
    return lax.dot_general(
        gradients, weights_block, (((1,), (1,)), ((), ())), preferred_element_type=jnp.float32
    )


def weight_term(operand, gradients):
    return lax.dot_general(
        operand, gradients, (((0,), (0,)), ((), ())), preferred_element_type=jnp.float32
    )


def on_device(frames, retention, first_conv, second_conv, cotangent):
    both_full = gather_weights(jnp.stack([first_conv, second_conv]))
    first_full, second_full = both_full[0], both_full[1]
    payload_elements = frames[0].astype(jnp.float32)
    keep_rate = retention[0]
    length, channels = payload_elements.shape
    short_lag = length // 4
    (local_last,) = drift(keep_rate, payload_elements, jnp.zeros((1, channels), jnp.float32), False)
    factor_last = jnp.prod(keep_rate, axis=0)
    carried = carried_level(jnp.stack([factor_last, local_last[0]]), 16)
    removed, _ = drift(keep_rate, payload_elements, carried[None, :], True)
    trend_removed = removed.astype(jnp.bfloat16)
    tail_rows = trend_removed[length - short_lag :]
    near_tail = passed_along(tail_rows, TM, 1)
    own_past = jnp.concatenate([near_tail, trend_removed[: length - short_lag]], axis=0)
    opening_layer_input = jnp.concatenate([own_past, trend_removed], axis=1)
    stacked_pre = accumulate_with(
        opening_layer_input, first_full
    )
    stacked_out = (trend_removed.astype(jnp.float32) + gated(stacked_pre)).astype(jnp.bfloat16)
    earlier_out = passed_along(stacked_out, TM, 1)
    closing_layer_input = jnp.concatenate([earlier_out, stacked_out], axis=1)
    second_pre = accumulate_with(
        closing_layer_input, second_full
    )
    top_hidden = (stacked_out.astype(jnp.float32) + gated(second_pre)).astype(jnp.bfloat16)
    incoming_gradient = cotangent[0].astype(jnp.float32)
    second_grad = gate_grad(second_pre, incoming_gradient).astype(jnp.bfloat16)
    second_term = weight_term(closing_layer_input, second_grad)
    closing_backward = back_with(
        second_grad, second_full
    )
    carried_back = passed_along(
        closing_backward[:, :channels].astype(jnp.bfloat16), TM, -1
    ).astype(jnp.float32)
    opening_upstream_gradient = incoming_gradient + closing_backward[:, channels:] + carried_back
    first_grad = gate_grad(stacked_pre, opening_upstream_gradient).astype(jnp.bfloat16)
    first_term = weight_term(opening_layer_input, first_grad)
    grads = reduce_gradients(jnp.stack([first_term, second_term]))
    grad_first, grad_second = grads[0], grads[1]
    return (top_hidden[None], grad_first, grad_second)


def solution(mesh):
    tm, fsdp = mesh.shape["tm"], mesh.shape["fsdp"]
    split = mesh.devices.reshape(tm // 2, 2, 4, fsdp // 8, 2)
    sub = Mesh(split, SUB_AXES)
    rows, frames = ("x", "y", "zh"), TM
    in_specs = (
        P(rows, frames, None),
        P(rows, frames, None),
        P(rows, None),
        P(rows, None),
        P(rows, frames, None),
    )
    out_specs = (P(rows, frames, None), P(rows, None), P(rows, None))
    return jax.shard_map(
        on_device, mesh=sub, in_specs=in_specs, out_specs=out_specs, check_vma=False
    )
```

```python
import jax
import jax.numpy as jnp
from jax import lax
from jax.experimental import pallas as pl
from jax.sharding import Mesh, PartitionSpec as P


def passed_along(value, axis, steps):
    count = 16
    leading, last = (max(0, -steps), min(count, count - steps))
    return lax.ppermute(value, axis, [(source, source + steps) for source in range(leading, last)])


TM = ("zl", "c")
SUB_AXES = ("zl", "c", "x", "y", "zh")


def rotated(value, axis, size, steps):
    return lax.ppermute(value, axis, [(i, (i + steps) % size) for i in range(size)])


def gather_over(block, axis, size, dim):
    place = lax.axis_index(axis)
    width = block.shape[dim]
    shape = list(block.shape)
    shape[dim] = width * size
    out = lax.dynamic_update_slice_in_dim(jnp.zeros(shape, block.dtype), block, place * width, dim)
    for steps in range(1, size):
        arrived = rotated(block, axis, size, steps)
        out = lax.dynamic_update_slice_in_dim(out, arrived, ((place - steps) % size) * width, dim)
    return out


def scatter_over(total, axis, size, dim):
    place = lax.axis_index(axis)
    width = total.shape[dim] // size
    sent = total.astype(jnp.bfloat16)
    acc = lax.dynamic_slice_in_dim(total, place * width, width, dim).astype(jnp.float32)
    for steps in range(1, size):
        piece = lax.dynamic_slice_in_dim(sent, ((place + steps) % size) * width, width, dim)
        acc = acc + rotated(piece, axis, size, steps).astype(jnp.float32)
    return acc


def summed_over(total, axis, size):
    stride = 1
    while stride < size:
        partner = lax.ppermute(total, axis, [(i, i ^ stride) for i in range(size)])
        total = total + partner
        stride *= 2
    return total


def gather_weight(shard):
    core = lax.axis_index("c")
    half = shard.shape[2] // 2
    mine = lax.dynamic_slice_in_dim(shard, core * half, half, 2)
    rows = gather_over(gather_over(gather_over(mine, "zh", 2, 1), "y", 4, 1), "x", 4, 1)
    return gather_over(rows, "c", 2, 2)


def reduce_gradient(partial):
    partial = partial.astype(jnp.bfloat16)
    cols = scatter_over(partial, "c", 2, 2)
    rows = scatter_over(scatter_over(scatter_over(cols, "x", 4, 1), "y", 4, 1), "zh", 2, 1)
    total = summed_over(rows, "zl", 8)
    return gather_over(total, "c", 2, 2)


def drift_body(emit, rate_ref, value_ref, start_ref, *out_refs):
    rows = rate_ref.shape[0]

    def block(b, level):
        base = pl.multiple_of(b * 8, 8)
        rate = rate_ref[pl.ds(base, 8), :]
        value = value_ref[pl.ds(base, 8), :]
        for i in range(8):
            keep = rate[i : i + 1, :]
            level = keep * level + (1.0 - keep) * value[i : i + 1, :]
            if emit:
                out_refs[0][pl.ds(base + i, 1), :] = value[i : i + 1, :] - level
        return level

    out_refs[-1][...] = lax.fori_loop(0, rows // 8, block, start_ref[...])


def drift(rate, value, start, emit):
    rows, channels = rate.shape
    outs = [jax.ShapeDtypeStruct((1, channels), jnp.float32)]
    if emit:
        outs = [jax.ShapeDtypeStruct((rows, channels), jnp.float32)] + outs
    return pl.pallas_call(lambda *refs: drift_body(emit, *refs), out_shape=outs)(rate, value, start)


def spread_over(block, axis, count):
    copies = jnp.broadcast_to(block[None], (count,) + block.shape)
    return lax.all_to_all(copies, axis, 0, 0, tiled=True)


def carried_level(state, size):
    place = lax.axis_index(TM)
    every = spread_over(state, TM, size)
    level = jnp.ones_like(state[0]), jnp.zeros_like(state[1])
    for source in range(size - 1):
        joined = combine_maps(level, (every[source, 0], every[source, 1]))
        level = tuple(jnp.where(source < place, j, l) for j, l in zip(joined, level))
    return level[1]


def combine_maps(earlier, later):
    return (earlier[0] * later[0], later[0] * earlier[1] + later[1])


def gated(pre_values):
    split_at = pre_values.shape[1] // 2
    return jnp.tanh(pre_values[:, :split_at]) * jax.nn.sigmoid(pre_values[:, split_at:])


def gate_grad(pre_values, incoming_gradient):
    split_at = pre_values.shape[1] // 2
    tanh_part = jnp.tanh(pre_values[:, :split_at])
    gate_part = jax.nn.sigmoid(pre_values[:, split_at:])
    return jnp.concatenate(
        [
            incoming_gradient * gate_part * (1.0 - tanh_part * tanh_part),
            incoming_gradient * tanh_part * gate_part * (1.0 - gate_part),
        ],
        axis=1,
    )


def accumulate_with(operand, weights_block):
    return jnp.dot(operand, weights_block, preferred_element_type=jnp.float32)


def back_with(gradients, weights_block):
    return lax.dot_general(
        gradients, weights_block, (((1,), (1,)), ((), ())), preferred_element_type=jnp.float32
    )


def weight_term(operand, gradients):
    return lax.dot_general(
        operand, gradients, (((0,), (0,)), ((), ())), preferred_element_type=jnp.float32
    )


def on_device(frames, retention, first_conv, second_conv, cotangent):
    both_full = gather_weight(jnp.stack([first_conv, second_conv]))
    first_full, second_full = both_full[0], both_full[1]
    payload_elements = frames[0].astype(jnp.float32)
    keep_rate = retention[0]
    length, channels = payload_elements.shape
    short_lag = length // 4
    (local_last,) = drift(keep_rate, payload_elements, jnp.zeros((1, channels), jnp.float32), False)
    factor_last = jnp.prod(keep_rate, axis=0)
    carried = carried_level(jnp.stack([factor_last, local_last[0]]), 16)
    removed, _ = drift(keep_rate, payload_elements, carried[None, :], True)
    trend_removed = removed.astype(jnp.bfloat16)
    tail_rows = trend_removed[length - short_lag :]
    near_tail = passed_along(tail_rows, TM, 1)
    own_past = jnp.concatenate([near_tail, trend_removed[: length - short_lag]], axis=0)
    opening_layer_input = jnp.concatenate([own_past, trend_removed], axis=1)
    stacked_pre = accumulate_with(
        opening_layer_input, first_full
    )
    stacked_out = (trend_removed.astype(jnp.float32) + gated(stacked_pre)).astype(jnp.bfloat16)
    earlier_out = passed_along(stacked_out, TM, 1)
    closing_layer_input = jnp.concatenate([earlier_out, stacked_out], axis=1)
    second_pre = accumulate_with(
        closing_layer_input, second_full
    )
    top_hidden = (stacked_out.astype(jnp.float32) + gated(second_pre)).astype(jnp.bfloat16)
    incoming_gradient = cotangent[0].astype(jnp.float32)
    second_grad = gate_grad(second_pre, incoming_gradient).astype(jnp.bfloat16)
    second_term = weight_term(closing_layer_input, second_grad)
    closing_backward = back_with(
        second_grad, second_full
    )
    carried_back = passed_along(
        closing_backward[:, :channels].astype(jnp.bfloat16), TM, -1
    ).astype(jnp.float32)
    opening_upstream_gradient = incoming_gradient + closing_backward[:, channels:] + carried_back
    first_grad = gate_grad(stacked_pre, opening_upstream_gradient).astype(jnp.bfloat16)
    first_term = weight_term(opening_layer_input, first_grad)
    grads = reduce_gradient(jnp.stack([first_term, second_term]))
    grad_first, grad_second = grads[0], grads[1]
    return (top_hidden[None], grad_first, grad_second)


def solution(mesh):
    tm, fsdp = mesh.shape["tm"], mesh.shape["fsdp"]
    split = mesh.devices.reshape(tm // 2, 2, 4, fsdp // 8, 2)
    sub = Mesh(split, SUB_AXES)
    rows, frames = ("x", "y", "zh"), TM
    in_specs = (
        P(rows, frames, None),
        P(rows, frames, None),
        P(rows, None),
        P(rows, None),
        P(rows, frames, None),
    )
    out_specs = (P(rows, frames, None), P(rows, None), P(rows, None))
    return jax.shard_map(
        on_device, mesh=sub, in_specs=in_specs, out_specs=out_specs, check_vma=False
    )
```

```python
import jax
import jax.numpy as jnp
from jax import lax
from jax.experimental import pallas as pl
from jax.sharding import Mesh, PartitionSpec as P


def passed_along(value, axis, steps):
    count = 16
    leading, last = (max(0, -steps), min(count, count - steps))
    return lax.ppermute(value, axis, [(source, source + steps) for source in range(leading, last)])


TM = ("zl", "c")
SUB_AXES = ("zl", "c", "x", "y", "zh")


def rotated(value, axis, size, steps):
    return lax.ppermute(value, axis, [(i, (i + steps) % size) for i in range(size)])


def gather_over(block, axis, size, dim):
    place = lax.axis_index(axis)
    width = block.shape[dim]
    shape = list(block.shape)
    shape[dim] = width * size
    out = lax.dynamic_update_slice_in_dim(jnp.zeros(shape, block.dtype), block, place * width, dim)
    for steps in range(1, size):
        arrived = rotated(block, axis, size, steps)
        out = lax.dynamic_update_slice_in_dim(out, arrived, ((place - steps) % size) * width, dim)
    return out


def scatter_over(total, axis, size, dim):
    place = lax.axis_index(axis)
    width = total.shape[dim] // size
    sent = total.astype(jnp.bfloat16)
    acc = lax.dynamic_slice_in_dim(total, place * width, width, dim).astype(jnp.float32)
    for steps in range(1, size):
        piece = lax.dynamic_slice_in_dim(sent, ((place + steps) % size) * width, width, dim)
        acc = acc + rotated(piece, axis, size, steps).astype(jnp.float32)
    return acc


def summed_over(total, axis, size):
    stride = 1
    while stride < size:
        partner = lax.ppermute(total, axis, [(i, i ^ stride) for i in range(size)])
        total = total + partner
        stride *= 2
    return total


def gather_weight(shard, ready):
    core = lax.axis_index("c")
    half = shard.shape[2] // 2
    mine = lax.dynamic_slice_in_dim(shard, core * half, half, 2)
    rows = gather_over(gather_over(mine, "zh", 2, 1), "y", 4, 1)
    rows, ready = lax.optimization_barrier((rows, ready))
    rows = gather_over(rows, "x", 4, 1)
    return gather_over(rows, "c", 2, 2), ready


def reduce_gradient(partial):
    partial = partial.astype(jnp.bfloat16)
    cols = scatter_over(partial, "c", 2, 2)
    rows = scatter_over(scatter_over(scatter_over(cols, "x", 4, 1), "y", 4, 1), "zh", 2, 1)
    total = summed_over(rows, "zl", 8)
    return gather_over(total, "c", 2, 2)


def drift_body(emit, rate_ref, value_ref, start_ref, *out_refs):
    rows = rate_ref.shape[0]

    def block(b, level):
        base = pl.multiple_of(b * 8, 8)
        rate = rate_ref[pl.ds(base, 8), :]
        value = value_ref[pl.ds(base, 8), :]
        for i in range(8):
            keep = rate[i : i + 1, :]
            level = keep * level + (1.0 - keep) * value[i : i + 1, :]
            if emit:
                out_refs[0][pl.ds(base + i, 1), :] = value[i : i + 1, :] - level
        return level

    out_refs[-1][...] = lax.fori_loop(0, rows // 8, block, start_ref[...])


def drift(rate, value, start, emit):
    rows, channels = rate.shape
    outs = [jax.ShapeDtypeStruct((1, channels), jnp.float32)]
    if emit:
        outs = [jax.ShapeDtypeStruct((rows, channels), jnp.float32)] + outs
    return pl.pallas_call(lambda *refs: drift_body(emit, *refs), out_shape=outs)(rate, value, start)


def spread_over(block, axis, count):
    copies = jnp.broadcast_to(block[None], (count,) + block.shape)
    return lax.all_to_all(copies, axis, 0, 0, tiled=True)


def carried_level(state, size):
    place = lax.axis_index(TM)
    every = spread_over(state, TM, size)
    level = jnp.ones_like(state[0]), jnp.zeros_like(state[1])
    for source in range(size - 1):
        joined = combine_maps(level, (every[source, 0], every[source, 1]))
        level = tuple(jnp.where(source < place, j, l) for j, l in zip(joined, level))
    return level[1]


def combine_maps(earlier, later):
    return (earlier[0] * later[0], later[0] * earlier[1] + later[1])


def gated(pre_values):
    split_at = pre_values.shape[1] // 2
    return jnp.tanh(pre_values[:, :split_at]) * jax.nn.sigmoid(pre_values[:, split_at:])


def gate_grad(pre_values, incoming_gradient):
    split_at = pre_values.shape[1] // 2
    tanh_part = jnp.tanh(pre_values[:, :split_at])
    gate_part = jax.nn.sigmoid(pre_values[:, split_at:])
    return jnp.concatenate(
        [
            incoming_gradient * gate_part * (1.0 - tanh_part * tanh_part),
            incoming_gradient * tanh_part * gate_part * (1.0 - gate_part),
        ],
        axis=1,
    )


def accumulate_with(operand, weights_block):
    return jnp.dot(operand, weights_block, preferred_element_type=jnp.float32)


def back_with(gradients, weights_block):
    return lax.dot_general(
        gradients, weights_block, (((1,), (1,)), ((), ())), preferred_element_type=jnp.float32
    )


def weight_term(operand, gradients):
    return lax.dot_general(
        operand, gradients, (((0,), (0,)), ((), ())), preferred_element_type=jnp.float32
    )


def on_device(frames, retention, first_conv, second_conv, cotangent):
    payload_elements = frames[0].astype(jnp.float32)
    keep_rate = retention[0]
    length, channels = payload_elements.shape
    short_lag = length // 4
    (local_last,) = drift(keep_rate, payload_elements, jnp.zeros((1, channels), jnp.float32), False)
    factor_last = jnp.prod(keep_rate, axis=0)
    state = jnp.stack([factor_last, local_last[0]])
    state, shards = lax.optimization_barrier((state, jnp.stack([first_conv, second_conv])))
    carried = carried_level(state, 16)
    both_full, carried = gather_weight(shards, carried)
    first_full, second_full = both_full[0], both_full[1]
    removed, _ = drift(keep_rate, payload_elements, carried[None, :], True)
    trend_removed = removed.astype(jnp.bfloat16)
    tail_rows = trend_removed[length - short_lag :]
    near_tail = passed_along(tail_rows, TM, 1)
    own_past = jnp.concatenate([near_tail, trend_removed[: length - short_lag]], axis=0)
    opening_layer_input = jnp.concatenate([own_past, trend_removed], axis=1)
    stacked_pre = accumulate_with(
        opening_layer_input, first_full
    )
    stacked_out = (trend_removed.astype(jnp.float32) + gated(stacked_pre)).astype(jnp.bfloat16)
    earlier_out = passed_along(stacked_out, TM, 1)
    closing_layer_input = jnp.concatenate([earlier_out, stacked_out], axis=1)
    second_pre = accumulate_with(
        closing_layer_input, second_full
    )
    top_hidden = (stacked_out.astype(jnp.float32) + gated(second_pre)).astype(jnp.bfloat16)
    incoming_gradient = cotangent[0].astype(jnp.float32)
    second_grad = gate_grad(second_pre, incoming_gradient).astype(jnp.bfloat16)
    second_term = weight_term(closing_layer_input, second_grad)
    closing_backward = back_with(
        second_grad, second_full
    )
    carried_back = passed_along(
        closing_backward[:, :channels].astype(jnp.bfloat16), TM, -1
    ).astype(jnp.float32)
    opening_upstream_gradient = incoming_gradient + closing_backward[:, channels:] + carried_back
    first_grad = gate_grad(stacked_pre, opening_upstream_gradient).astype(jnp.bfloat16)
    first_term = weight_term(opening_layer_input, first_grad)
    grads = reduce_gradient(jnp.stack([first_term, second_term]))
    grad_first, grad_second = grads[0], grads[1]
    return (top_hidden[None], grad_first, grad_second)


def solution(mesh):
    tm, fsdp = mesh.shape["tm"], mesh.shape["fsdp"]
    split = mesh.devices.reshape(tm // 2, 2, 4, fsdp // 8, 2)
    sub = Mesh(split, SUB_AXES)
    rows, frames = ("x", "y", "zh"), TM
    in_specs = (
        P(rows, frames, None),
        P(rows, frames, None),
        P(rows, None),
        P(rows, None),
        P(rows, frames, None),
    )
    out_specs = (P(rows, frames, None), P(rows, None), P(rows, None))
    return jax.shard_map(
        on_device, mesh=sub, in_specs=in_specs, out_specs=out_specs, check_vma=False
    )
```

```python
import jax
import jax.numpy as jnp
from jax import lax
from jax.experimental import pallas as pl
from jax.sharding import Mesh, PartitionSpec as P


def passed_along(value, axis, steps):
    count = 16
    leading, last = (max(0, -steps), min(count, count - steps))
    return lax.ppermute(value, axis, [(source, source + steps) for source in range(leading, last)])


TM = ("zl", "c")
SUB_AXES = ("zl", "c", "x", "y", "zh")


def rotated(value, axis, size, steps):
    return lax.ppermute(value, axis, [(i, (i + steps) % size) for i in range(size)])


def gather_over(block, axis, size, dim):
    place = lax.axis_index(axis)
    width = block.shape[dim]
    shape = list(block.shape)
    shape[dim] = width * size
    out = lax.dynamic_update_slice_in_dim(jnp.zeros(shape, block.dtype), block, place * width, dim)
    for steps in range(1, size):
        arrived = rotated(block, axis, size, steps)
        out = lax.dynamic_update_slice_in_dim(out, arrived, ((place - steps) % size) * width, dim)
    return out


def scatter_over(total, axis, size, dim):
    place = lax.axis_index(axis)
    width = total.shape[dim] // size
    sent = total.astype(jnp.bfloat16)
    acc = lax.dynamic_slice_in_dim(total, place * width, width, dim).astype(jnp.float32)
    for steps in range(1, size):
        piece = lax.dynamic_slice_in_dim(sent, ((place + steps) % size) * width, width, dim)
        acc = acc + rotated(piece, axis, size, steps).astype(jnp.float32)
    return acc


def summed_over(total, axis, size):
    stride = 1
    while stride < size:
        partner = lax.ppermute(total, axis, [(i, i ^ stride) for i in range(size)])
        total = total + partner
        stride *= 2
    return total


def halves(value, dim):
    half = value.shape[dim] // 2
    return lax.slice_in_dim(value, 0, half, axis=dim), lax.slice_in_dim(value, half, 2 * half, axis=dim)


def gather_ring4(block, axis, dim, half_dim):
    place = lax.axis_index(axis)
    width = block.shape[dim]
    shape = list(block.shape)
    shape[dim] = width * 4
    out = lax.dynamic_update_slice_in_dim(jnp.zeros(shape, block.dtype), block, place * width, dim)
    from_left = rotated(block, axis, 4, 1)
    from_right = rotated(block, axis, 4, -1)
    out = lax.dynamic_update_slice_in_dim(out, from_left, ((place - 1) % 4) * width, dim)
    out = lax.dynamic_update_slice_in_dim(out, from_right, ((place + 1) % 4) * width, dim)
    far_left = rotated(halves(from_left, half_dim)[0], axis, 4, 1)
    far_right = rotated(halves(from_right, half_dim)[1], axis, 4, -1)
    far = jnp.concatenate([far_left, far_right], axis=half_dim)
    return lax.dynamic_update_slice_in_dim(out, far, ((place + 2) % 4) * width, dim)


def scatter_ring4(total, axis, dim, half_dim):
    place = lax.axis_index(axis)
    width = total.shape[dim] // 4
    sent = total.astype(jnp.bfloat16)

    def part(source, steps):
        return halves(lax.dynamic_slice_in_dim(source, ((place + steps) % 4) * width, width, dim), half_dim)

    own = [h.astype(jnp.float32) for h in part(total, 0)]
    right_next, left_next = part(total, 1), part(total, -1)
    to_right = jnp.stack([part(sent, 1)[1], part(sent, 2)[0]])
    to_left = jnp.stack([part(sent, -1)[0], part(sent, 2)[1]])
    from_left = rotated(to_right, axis, 4, 1).astype(jnp.float32)
    from_right = rotated(to_left, axis, 4, -1).astype(jnp.float32)
    onward_right = (from_left[1] + right_next[0].astype(jnp.float32)).astype(jnp.bfloat16)
    onward_left = (from_right[1] + left_next[1].astype(jnp.float32)).astype(jnp.bfloat16)
    far_left = rotated(onward_right, axis, 4, 1).astype(jnp.float32)
    far_right = rotated(onward_left, axis, 4, -1).astype(jnp.float32)
    first = own[0] + from_right[0] + far_left
    second = own[1] + from_left[0] + far_right
    return jnp.concatenate([first, second], axis=half_dim)


def gather_weight(shard, ready):
    core = lax.axis_index("c")
    half = shard.shape[2] // 2
    mine = lax.dynamic_slice_in_dim(shard, core * half, half, 2)
    rows = gather_over(gather_over(mine, "zh", 2, 1), "y", 4, 1)
    rows, ready = lax.optimization_barrier((rows, ready))
    rows = gather_ring4(rows, "x", 1, 2)
    return gather_over(rows, "c", 2, 2), ready


def reduce_gradient(partial):
    partial = partial.astype(jnp.bfloat16)
    cols = scatter_over(partial, "c", 2, 2)
    rows = scatter_over(scatter_over(scatter_ring4(cols, "x", 1, 2), "y", 4, 1), "zh", 2, 1)
    total = summed_over(rows, "zl", 8)
    return gather_over(total, "c", 2, 2)


def drift_body(emit, rate_ref, value_ref, start_ref, *out_refs):
    rows = rate_ref.shape[0]

    def block(b, level):
        base = pl.multiple_of(b * 8, 8)
        rate = rate_ref[pl.ds(base, 8), :]
        value = value_ref[pl.ds(base, 8), :]
        for i in range(8):
            keep = rate[i : i + 1, :]
            level = keep * level + (1.0 - keep) * value[i : i + 1, :]
            if emit:
                out_refs[0][pl.ds(base + i, 1), :] = value[i : i + 1, :] - level
        return level

    out_refs[-1][...] = lax.fori_loop(0, rows // 8, block, start_ref[...])


def drift(rate, value, start, emit):
    rows, channels = rate.shape
    outs = [jax.ShapeDtypeStruct((1, channels), jnp.float32)]
    if emit:
        outs = [jax.ShapeDtypeStruct((rows, channels), jnp.float32)] + outs
    return pl.pallas_call(lambda *refs: drift_body(emit, *refs), out_shape=outs)(rate, value, start)


def spread_over(block, axis, count):
    copies = jnp.broadcast_to(block[None], (count,) + block.shape)
    return lax.all_to_all(copies, axis, 0, 0, tiled=True)


def carried_level(state, size):
    place = lax.axis_index(TM)
    every = spread_over(state, TM, size)
    level = jnp.ones_like(state[0]), jnp.zeros_like(state[1])
    for source in range(size - 1):
        joined = combine_maps(level, (every[source, 0], every[source, 1]))
        level = tuple(jnp.where(source < place, j, l) for j, l in zip(joined, level))
    return level[1]


def combine_maps(earlier, later):
    return (earlier[0] * later[0], later[0] * earlier[1] + later[1])


def gated(pre_values):
    split_at = pre_values.shape[1] // 2
    return jnp.tanh(pre_values[:, :split_at]) * jax.nn.sigmoid(pre_values[:, split_at:])


def gate_grad(pre_values, incoming_gradient):
    split_at = pre_values.shape[1] // 2
    tanh_part = jnp.tanh(pre_values[:, :split_at])
    gate_part = jax.nn.sigmoid(pre_values[:, split_at:])
    return jnp.concatenate(
        [
            incoming_gradient * gate_part * (1.0 - tanh_part * tanh_part),
            incoming_gradient * tanh_part * gate_part * (1.0 - gate_part),
        ],
        axis=1,
    )


def accumulate_with(operand, weights_block):
    return jnp.dot(operand, weights_block, preferred_element_type=jnp.float32)


def back_with(gradients, weights_block):
    return lax.dot_general(
        gradients, weights_block, (((1,), (1,)), ((), ())), preferred_element_type=jnp.float32
    )


def weight_term(operand, gradients):
    return lax.dot_general(
        operand, gradients, (((0,), (0,)), ((), ())), preferred_element_type=jnp.float32
    )


def on_device(frames, retention, first_conv, second_conv, cotangent):
    payload_elements = frames[0].astype(jnp.float32)
    keep_rate = retention[0]
    length, channels = payload_elements.shape
    short_lag = length // 4
    (local_last,) = drift(keep_rate, payload_elements, jnp.zeros((1, channels), jnp.float32), False)
    factor_last = jnp.prod(keep_rate, axis=0)
    state = jnp.stack([factor_last, local_last[0]])
    state, shards = lax.optimization_barrier((state, jnp.stack([first_conv, second_conv])))
    carried = carried_level(state, 16)
    both_full, carried = gather_weight(shards, carried)
    first_full, second_full = both_full[0], both_full[1]
    removed, _ = drift(keep_rate, payload_elements, carried[None, :], True)
    trend_removed = removed.astype(jnp.bfloat16)
    tail_rows = trend_removed[length - short_lag :]
    near_tail = passed_along(tail_rows, TM, 1)
    own_past = jnp.concatenate([near_tail, trend_removed[: length - short_lag]], axis=0)
    opening_layer_input = jnp.concatenate([own_past, trend_removed], axis=1)
    stacked_pre = accumulate_with(
        opening_layer_input, first_full
    )
    stacked_out = (trend_removed.astype(jnp.float32) + gated(stacked_pre)).astype(jnp.bfloat16)
    earlier_out = passed_along(stacked_out, TM, 1)
    closing_layer_input = jnp.concatenate([earlier_out, stacked_out], axis=1)
    second_pre = accumulate_with(
        closing_layer_input, second_full
    )
    top_hidden = (stacked_out.astype(jnp.float32) + gated(second_pre)).astype(jnp.bfloat16)
    incoming_gradient = cotangent[0].astype(jnp.float32)
    second_grad = gate_grad(second_pre, incoming_gradient).astype(jnp.bfloat16)
    second_term = weight_term(closing_layer_input, second_grad)
    closing_backward = back_with(
        second_grad, second_full
    )
    carried_back = passed_along(
        closing_backward[:, :channels].astype(jnp.bfloat16), TM, -1
    ).astype(jnp.float32)
    opening_upstream_gradient = incoming_gradient + closing_backward[:, channels:] + carried_back
    first_grad = gate_grad(stacked_pre, opening_upstream_gradient).astype(jnp.bfloat16)
    first_term = weight_term(opening_layer_input, first_grad)
    grads = reduce_gradient(jnp.stack([first_term, second_term]))
    grad_first, grad_second = grads[0], grads[1]
    return (top_hidden[None], grad_first, grad_second)


def solution(mesh):
    tm, fsdp = mesh.shape["tm"], mesh.shape["fsdp"]
    split = mesh.devices.reshape(tm // 2, 2, 4, fsdp // 8, 2)
    sub = Mesh(split, SUB_AXES)
    rows, frames = ("x", "y", "zh"), TM
    in_specs = (
        P(rows, frames, None),
        P(rows, frames, None),
        P(rows, None),
        P(rows, None),
        P(rows, frames, None),
    )
    out_specs = (P(rows, frames, None), P(rows, None), P(rows, None))
    return jax.shard_map(
        on_device, mesh=sub, in_specs=in_specs, out_specs=out_specs, check_vma=False
    )
```

```python
import jax
import jax.numpy as jnp
from jax import lax
from jax.experimental import pallas as pl
from jax.sharding import Mesh, PartitionSpec as P


def passed_along(value, axis, steps):
    count = 16
    leading, last = (max(0, -steps), min(count, count - steps))
    return lax.ppermute(value, axis, [(source, source + steps) for source in range(leading, last)])


TM = ("zl", "c")
SUB_AXES = ("zl", "c", "x", "y", "zh")


def rotated(value, axis, size, steps):
    return lax.ppermute(value, axis, [(i, (i + steps) % size) for i in range(size)])


def farthest_first(size):
    return sorted(range(1, size), key=lambda steps: -min(steps, size - steps))


def gather_over(block, axis, size, dim):
    place = lax.axis_index(axis)
    width = block.shape[dim]
    shape = list(block.shape)
    shape[dim] = width * size
    out = lax.dynamic_update_slice_in_dim(jnp.zeros(shape, block.dtype), block, place * width, dim)
    for steps in farthest_first(size):
        arrived = rotated(block, axis, size, steps)
        out = lax.dynamic_update_slice_in_dim(out, arrived, ((place - steps) % size) * width, dim)
    return out


def scatter_over(total, axis, size, dim):
    place = lax.axis_index(axis)
    width = total.shape[dim] // size
    sent = total.astype(jnp.bfloat16)
    acc = lax.dynamic_slice_in_dim(total, place * width, width, dim).astype(jnp.float32)
    for steps in farthest_first(size):
        piece = lax.dynamic_slice_in_dim(sent, ((place + steps) % size) * width, width, dim)
        acc = acc + rotated(piece, axis, size, steps).astype(jnp.float32)
    return acc


def summed_over(total, axis, size):
    stride = 1
    while stride < size:
        partner = lax.ppermute(total, axis, [(i, i ^ stride) for i in range(size)])
        total = total + partner
        stride *= 2
    return total


def gather_weight(shard, ready):
    core = lax.axis_index("c")
    half = shard.shape[2] // 2
    mine = lax.dynamic_slice_in_dim(shard, core * half, half, 2)
    rows = gather_over(gather_over(mine, "zh", 2, 1), "y", 4, 1)
    rows, ready = lax.optimization_barrier((rows, ready))
    rows = gather_over(rows, "x", 4, 1)
    return gather_over(rows, "c", 2, 2), ready


def reduce_gradient(partial):
    partial = partial.astype(jnp.bfloat16)
    cols = scatter_over(partial, "c", 2, 2)
    rows = scatter_over(scatter_over(scatter_over(cols, "x", 4, 1), "y", 4, 1), "zh", 2, 1)
    total = summed_over(rows, "zl", 8)
    return gather_over(total, "c", 2, 2)


def drift_body(emit, rate_ref, value_ref, start_ref, *out_refs):
    rows = rate_ref.shape[0]

    def block(b, level):
        base = pl.multiple_of(b * 8, 8)
        rate = rate_ref[pl.ds(base, 8), :]
        value = value_ref[pl.ds(base, 8), :]
        for i in range(8):
            keep = rate[i : i + 1, :]
            level = keep * level + (1.0 - keep) * value[i : i + 1, :]
            if emit:
                out_refs[0][pl.ds(base + i, 1), :] = value[i : i + 1, :] - level
        return level

    out_refs[-1][...] = lax.fori_loop(0, rows // 8, block, start_ref[...])


def drift(rate, value, start, emit):
    rows, channels = rate.shape
    outs = [jax.ShapeDtypeStruct((1, channels), jnp.float32)]
    if emit:
        outs = [jax.ShapeDtypeStruct((rows, channels), jnp.float32)] + outs
    return pl.pallas_call(lambda *refs: drift_body(emit, *refs), out_shape=outs)(rate, value, start)


def spread_over(block, axis, count):
    copies = jnp.broadcast_to(block[None], (count,) + block.shape)
    return lax.all_to_all(copies, axis, 0, 0, tiled=True)


def carried_level(state, size):
    place = lax.axis_index(TM)
    every = spread_over(state, TM, size)
    level = jnp.ones_like(state[0]), jnp.zeros_like(state[1])
    for source in range(size - 1):
        joined = combine_maps(level, (every[source, 0], every[source, 1]))
        level = tuple(jnp.where(source < place, j, l) for j, l in zip(joined, level))
    return level[1]


def combine_maps(earlier, later):
    return (earlier[0] * later[0], later[0] * earlier[1] + later[1])


def gated(pre_values):
    split_at = pre_values.shape[1] // 2
    return jnp.tanh(pre_values[:, :split_at]) * jax.nn.sigmoid(pre_values[:, split_at:])


def gate_grad(pre_values, incoming_gradient):
    split_at = pre_values.shape[1] // 2
    tanh_part = jnp.tanh(pre_values[:, :split_at])
    gate_part = jax.nn.sigmoid(pre_values[:, split_at:])
    return jnp.concatenate(
        [
            incoming_gradient * gate_part * (1.0 - tanh_part * tanh_part),
            incoming_gradient * tanh_part * gate_part * (1.0 - gate_part),
        ],
        axis=1,
    )


def accumulate_with(operand, weights_block):
    return jnp.dot(operand, weights_block, preferred_element_type=jnp.float32)


def back_with(gradients, weights_block):
    return lax.dot_general(
        gradients, weights_block, (((1,), (1,)), ((), ())), preferred_element_type=jnp.float32
    )


def weight_term(operand, gradients):
    return lax.dot_general(
        operand, gradients, (((0,), (0,)), ((), ())), preferred_element_type=jnp.float32
    )


def on_device(frames, retention, first_conv, second_conv, cotangent):
    payload_elements = frames[0].astype(jnp.float32)
    keep_rate = retention[0]
    length, channels = payload_elements.shape
    short_lag = length // 4
    (local_last,) = drift(keep_rate, payload_elements, jnp.zeros((1, channels), jnp.float32), False)
    factor_last = jnp.prod(keep_rate, axis=0)
    state = jnp.stack([factor_last, local_last[0]])
    state, shards = lax.optimization_barrier((state, jnp.stack([first_conv, second_conv])))
    carried = carried_level(state, 16)
    both_full, carried = gather_weight(shards, carried)
    first_full, second_full = both_full[0], both_full[1]
    removed, _ = drift(keep_rate, payload_elements, carried[None, :], True)
    trend_removed = removed.astype(jnp.bfloat16)
    tail_rows = trend_removed[length - short_lag :]
    near_tail = passed_along(tail_rows, TM, 1)
    own_past = jnp.concatenate([near_tail, trend_removed[: length - short_lag]], axis=0)
    opening_layer_input = jnp.concatenate([own_past, trend_removed], axis=1)
    stacked_pre = accumulate_with(
        opening_layer_input, first_full
    )
    stacked_out = (trend_removed.astype(jnp.float32) + gated(stacked_pre)).astype(jnp.bfloat16)
    earlier_out = passed_along(stacked_out, TM, 1)
    closing_layer_input = jnp.concatenate([earlier_out, stacked_out], axis=1)
    second_pre = accumulate_with(
        closing_layer_input, second_full
    )
    top_hidden = (stacked_out.astype(jnp.float32) + gated(second_pre)).astype(jnp.bfloat16)
    incoming_gradient = cotangent[0].astype(jnp.float32)
    second_grad = gate_grad(second_pre, incoming_gradient).astype(jnp.bfloat16)
    second_term = weight_term(closing_layer_input, second_grad)
    closing_backward = back_with(
        second_grad, second_full
    )
    carried_back = passed_along(
        closing_backward[:, :channels].astype(jnp.bfloat16), TM, -1
    ).astype(jnp.float32)
    opening_upstream_gradient = incoming_gradient + closing_backward[:, channels:] + carried_back
    first_grad = gate_grad(stacked_pre, opening_upstream_gradient).astype(jnp.bfloat16)
    first_term = weight_term(opening_layer_input, first_grad)
    grads = reduce_gradient(jnp.stack([first_term, second_term]))
    grad_first, grad_second = grads[0], grads[1]
    return (top_hidden[None], grad_first, grad_second)


def solution(mesh):
    tm, fsdp = mesh.shape["tm"], mesh.shape["fsdp"]
    split = mesh.devices.reshape(tm // 2, 2, 4, fsdp // 8, 2)
    sub = Mesh(split, SUB_AXES)
    rows, frames = ("x", "y", "zh"), TM
    in_specs = (
        P(rows, frames, None),
        P(rows, frames, None),
        P(rows, None),
        P(rows, None),
        P(rows, frames, None),
    )
    out_specs = (P(rows, frames, None), P(rows, None), P(rows, None))
    return jax.shard_map(
        on_device, mesh=sub, in_specs=in_specs, out_specs=out_specs, check_vma=False
    )
```

```python
import jax
import jax.numpy as jnp
from jax import lax
from jax.experimental import pallas as pl
from jax.sharding import Mesh, PartitionSpec as P


def passed_along(value, axis, steps):
    count = 16
    leading, last = (max(0, -steps), min(count, count - steps))
    return lax.ppermute(value, axis, [(source, source + steps) for source in range(leading, last)])


TM = ("zl", "c")
SUB_AXES = ("zl", "c", "x", "y", "zh")


def rotated(value, axis, size, steps):
    return lax.ppermute(value, axis, [(i, (i + steps) % size) for i in range(size)])


def farthest_first(size):
    return sorted(range(1, size), key=lambda steps: -min(steps, size - steps))


def gather_over(block, axis, size, dim):
    place = lax.axis_index(axis)
    width = block.shape[dim]
    shape = list(block.shape)
    shape[dim] = width * size
    out = lax.dynamic_update_slice_in_dim(jnp.zeros(shape, block.dtype), block, place * width, dim)
    for steps in farthest_first(size):
        arrived = rotated(block, axis, size, steps)
        out = lax.dynamic_update_slice_in_dim(out, arrived, ((place - steps) % size) * width, dim)
    return out


def scatter_over(total, axis, size, dim):
    place = lax.axis_index(axis)
    width = total.shape[dim] // size
    sent = total.astype(jnp.bfloat16)
    acc = lax.dynamic_slice_in_dim(total, place * width, width, dim).astype(jnp.float32)
    for steps in farthest_first(size):
        piece = lax.dynamic_slice_in_dim(sent, ((place + steps) % size) * width, width, dim)
        acc = acc + rotated(piece, axis, size, steps).astype(jnp.float32)
    return acc


def summed_over(total, axis, size):
    stride = 1
    while stride < size:
        partner = lax.ppermute(total, axis, [(i, i ^ stride) for i in range(size)])
        total = total + partner
        stride *= 2
    return total


def gather_weight(shard, ready):
    core = lax.axis_index("c")
    half = shard.shape[2] // 2
    mine = lax.dynamic_slice_in_dim(shard, core * half, half, 2)
    rows = gather_over(gather_over(mine, "zh", 2, 1), "y", 4, 1)
    rows, ready = lax.optimization_barrier((rows, ready))
    rows = gather_over(rows, "x", 4, 1)
    return gather_over(rows, "c", 2, 2), ready


def chip_half(partial):
    return scatter_over(partial.astype(jnp.bfloat16), "c", 2, 1)


def reduce_gradient(cols):
    rows = scatter_over(scatter_over(scatter_over(cols, "x", 4, 1), "y", 4, 1), "zh", 2, 1)
    total = summed_over(rows, "zl", 8)
    return gather_over(total, "c", 2, 2)


def drift_body(emit, rate_ref, value_ref, start_ref, *out_refs):
    rows = rate_ref.shape[0]

    def block(b, level):
        base = pl.multiple_of(b * 8, 8)
        rate = rate_ref[pl.ds(base, 8), :]
        value = value_ref[pl.ds(base, 8), :]
        for i in range(8):
            keep = rate[i : i + 1, :]
            level = keep * level + (1.0 - keep) * value[i : i + 1, :]
            if emit:
                out_refs[0][pl.ds(base + i, 1), :] = value[i : i + 1, :] - level
        return level

    out_refs[-1][...] = lax.fori_loop(0, rows // 8, block, start_ref[...])


def drift(rate, value, start, emit):
    rows, channels = rate.shape
    outs = [jax.ShapeDtypeStruct((1, channels), jnp.float32)]
    if emit:
        outs = [jax.ShapeDtypeStruct((rows, channels), jnp.float32)] + outs
    return pl.pallas_call(lambda *refs: drift_body(emit, *refs), out_shape=outs)(rate, value, start)


def spread_over(block, axis, count):
    copies = jnp.broadcast_to(block[None], (count,) + block.shape)
    return lax.all_to_all(copies, axis, 0, 0, tiled=True)


def carried_level(state, size):
    place = lax.axis_index(TM)
    every = spread_over(state, TM, size)
    level = jnp.ones_like(state[0]), jnp.zeros_like(state[1])
    for source in range(size - 1):
        joined = combine_maps(level, (every[source, 0], every[source, 1]))
        level = tuple(jnp.where(source < place, j, l) for j, l in zip(joined, level))
    return level[1]


def combine_maps(earlier, later):
    return (earlier[0] * later[0], later[0] * earlier[1] + later[1])


def gated(pre_values):
    split_at = pre_values.shape[1] // 2
    return jnp.tanh(pre_values[:, :split_at]) * jax.nn.sigmoid(pre_values[:, split_at:])


def gate_grad(pre_values, incoming_gradient):
    split_at = pre_values.shape[1] // 2
    tanh_part = jnp.tanh(pre_values[:, :split_at])
    gate_part = jax.nn.sigmoid(pre_values[:, split_at:])
    return jnp.concatenate(
        [
            incoming_gradient * gate_part * (1.0 - tanh_part * tanh_part),
            incoming_gradient * tanh_part * gate_part * (1.0 - gate_part),
        ],
        axis=1,
    )


def accumulate_with(operand, weights_block):
    return jnp.dot(operand, weights_block, preferred_element_type=jnp.float32)


def back_with(gradients, weights_block):
    return lax.dot_general(
        gradients, weights_block, (((1,), (1,)), ((), ())), preferred_element_type=jnp.float32
    )


def weight_term(operand, gradients):
    return lax.dot_general(
        operand, gradients, (((0,), (0,)), ((), ())), preferred_element_type=jnp.float32
    )


def on_device(frames, retention, first_conv, second_conv, cotangent):
    payload_elements = frames[0].astype(jnp.float32)
    keep_rate = retention[0]
    length, channels = payload_elements.shape
    short_lag = length // 4
    (local_last,) = drift(keep_rate, payload_elements, jnp.zeros((1, channels), jnp.float32), False)
    factor_last = jnp.prod(keep_rate, axis=0)
    state = jnp.stack([factor_last, local_last[0]])
    state, shards = lax.optimization_barrier((state, jnp.stack([first_conv, second_conv])))
    carried = carried_level(state, 16)
    both_full, carried = gather_weight(shards, carried)
    first_full, second_full = both_full[0], both_full[1]
    removed, _ = drift(keep_rate, payload_elements, carried[None, :], True)
    trend_removed = removed.astype(jnp.bfloat16)
    tail_rows = trend_removed[length - short_lag :]
    near_tail = passed_along(tail_rows, TM, 1)
    own_past = jnp.concatenate([near_tail, trend_removed[: length - short_lag]], axis=0)
    opening_layer_input = jnp.concatenate([own_past, trend_removed], axis=1)
    stacked_pre = accumulate_with(
        opening_layer_input, first_full
    )
    stacked_out = (trend_removed.astype(jnp.float32) + gated(stacked_pre)).astype(jnp.bfloat16)
    earlier_out = passed_along(stacked_out, TM, 1)
    closing_layer_input = jnp.concatenate([earlier_out, stacked_out], axis=1)
    second_pre = accumulate_with(
        closing_layer_input, second_full
    )
    top_hidden = (stacked_out.astype(jnp.float32) + gated(second_pre)).astype(jnp.bfloat16)
    incoming_gradient = cotangent[0].astype(jnp.float32)
    second_grad = gate_grad(second_pre, incoming_gradient).astype(jnp.bfloat16)
    second_cols = chip_half(weight_term(closing_layer_input, second_grad))
    closing_backward = back_with(
        second_grad, second_full
    )
    carried_back = passed_along(
        closing_backward[:, :channels].astype(jnp.bfloat16), TM, -1
    ).astype(jnp.float32)
    opening_upstream_gradient = incoming_gradient + closing_backward[:, channels:] + carried_back
    first_grad = gate_grad(stacked_pre, opening_upstream_gradient).astype(jnp.bfloat16)
    first_cols = chip_half(weight_term(opening_layer_input, first_grad))
    grads = reduce_gradient(jnp.stack([first_cols, second_cols]))
    grad_first, grad_second = grads[0], grads[1]
    return (top_hidden[None], grad_first, grad_second)


def solution(mesh):
    tm, fsdp = mesh.shape["tm"], mesh.shape["fsdp"]
    split = mesh.devices.reshape(tm // 2, 2, 4, fsdp // 8, 2)
    sub = Mesh(split, SUB_AXES)
    rows, frames = ("x", "y", "zh"), TM
    in_specs = (
        P(rows, frames, None),
        P(rows, frames, None),
        P(rows, None),
        P(rows, None),
        P(rows, frames, None),
    )
    out_specs = (P(rows, frames, None), P(rows, None), P(rows, None))
    return jax.shard_map(
        on_device, mesh=sub, in_specs=in_specs, out_specs=out_specs, check_vma=False
    )
```

```python
import jax
import jax.numpy as jnp
from jax import lax
from jax.experimental import pallas as pl
from jax.sharding import Mesh, PartitionSpec as P


def passed_along(value, axis, steps):
    count = 16
    leading, last = (max(0, -steps), min(count, count - steps))
    return lax.ppermute(value, axis, [(source, source + steps) for source in range(leading, last)])


TM = ("zl", "c")
SUB_AXES = ("zl", "c", "x", "y", "zh")


def rotated(value, axis, size, steps):
    return lax.ppermute(value, axis, [(i, (i + steps) % size) for i in range(size)])


def farthest_first(size):
    return sorted(range(1, size), key=lambda steps: -min(steps, size - steps))


def gather_over(block, axis, size, dim):
    place = lax.axis_index(axis)
    width = block.shape[dim]
    shape = list(block.shape)
    shape[dim] = width * size
    out = lax.dynamic_update_slice_in_dim(jnp.zeros(shape, block.dtype), block, place * width, dim)
    for steps in farthest_first(size):
        arrived = rotated(block, axis, size, steps)
        out = lax.dynamic_update_slice_in_dim(out, arrived, ((place - steps) % size) * width, dim)
    return out


def scatter_over(total, axis, size, dim):
    place = lax.axis_index(axis)
    width = total.shape[dim] // size
    sent = total.astype(jnp.bfloat16)
    acc = lax.dynamic_slice_in_dim(total, place * width, width, dim).astype(jnp.float32)
    for steps in farthest_first(size):
        piece = lax.dynamic_slice_in_dim(sent, ((place + steps) % size) * width, width, dim)
        acc = acc + rotated(piece, axis, size, steps).astype(jnp.float32)
    return acc


def summed_over(total, axis, size):
    stride = 1
    while stride < size:
        partner = lax.ppermute(total, axis, [(i, i ^ stride) for i in range(size)])
        total = total + partner
        stride *= 2
    return total


def crossed_pairs(steps, first):
    pairs = []
    for core in range(2):
        for x in range(4):
            for y in range(4):
                if (core == 0) == first:
                    target = (core, (x + steps) % 4, y)
                else:
                    target = (core, x, (y + steps) % 4)
                pairs.append((core * 16 + x * 4 + y, target[0] * 16 + target[1] * 4 + target[2]))
    return pairs


def crossed_place(first):
    core, x, y = lax.axis_index("c"), lax.axis_index("x"), lax.axis_index("y")
    return jnp.where((core == 0) == first, x, y)


def crossed_gather(block, first, dim):
    place = crossed_place(first)
    width = block.shape[dim]
    shape = list(block.shape)
    shape[dim] = width * 4
    out = lax.dynamic_update_slice_in_dim(jnp.zeros(shape, block.dtype), block, place * width, dim)
    for steps in farthest_first(4):
        arrived = lax.ppermute(block, ("c", "x", "y"), crossed_pairs(steps, first))
        out = lax.dynamic_update_slice_in_dim(out, arrived, ((place - steps) % 4) * width, dim)
    return out


def crossed_scatter(total, first, dim):
    place = crossed_place(first)
    width = total.shape[dim] // 4
    sent = total.astype(jnp.bfloat16)
    acc = lax.dynamic_slice_in_dim(total, place * width, width, dim).astype(jnp.float32)
    for steps in farthest_first(4):
        piece = lax.dynamic_slice_in_dim(sent, ((place + steps) % 4) * width, width, dim)
        arrived = lax.ppermute(piece, ("c", "x", "y"), crossed_pairs(steps, first))
        acc = acc + arrived.astype(jnp.float32)
    return acc


def core_order(blocks):
    swapped = jnp.swapaxes(blocks, 1, 2)
    return jnp.where(lax.axis_index("c") == 0, blocks, swapped)


def gather_weight(shard, ready):
    core = lax.axis_index("c")
    half = shard.shape[2] // 2
    mine = lax.dynamic_slice_in_dim(shard, core * half, half, 2)
    rows = gather_over(mine, "zh", 2, 1)
    count, block, width = rows.shape
    rows = crossed_gather(rows[:, None], False, 1)
    rows, ready = lax.optimization_barrier((rows, ready))
    rows = core_order(crossed_gather(rows[:, None], True, 1))
    rows = rows.reshape(count, 16 * block, width)
    return gather_over(rows, "c", 2, 2), ready


def chip_half(partial):
    return scatter_over(partial.astype(jnp.bfloat16), "c", 2, 1)


def reduce_gradient(cols):
    count, height, width = cols.shape
    blocks = core_order(cols.reshape(count, 4, 4, height // 16, width))
    blocks = crossed_scatter(crossed_scatter(blocks, True, 1), False, 2)
    rows = scatter_over(blocks.reshape(count, height // 16, width), "zh", 2, 1)
    total = summed_over(rows, "zl", 8)
    return gather_over(total, "c", 2, 2)


def drift_body(emit, rate_ref, value_ref, start_ref, *out_refs):
    rows = rate_ref.shape[0]

    def block(b, level):
        base = pl.multiple_of(b * 8, 8)
        rate = rate_ref[pl.ds(base, 8), :]
        value = value_ref[pl.ds(base, 8), :]
        for i in range(8):
            keep = rate[i : i + 1, :]
            level = keep * level + (1.0 - keep) * value[i : i + 1, :]
            if emit:
                out_refs[0][pl.ds(base + i, 1), :] = value[i : i + 1, :] - level
        return level

    out_refs[-1][...] = lax.fori_loop(0, rows // 8, block, start_ref[...])


def drift(rate, value, start, emit):
    rows, channels = rate.shape
    outs = [jax.ShapeDtypeStruct((1, channels), jnp.float32)]
    if emit:
        outs = [jax.ShapeDtypeStruct((rows, channels), jnp.float32)] + outs
    return pl.pallas_call(lambda *refs: drift_body(emit, *refs), out_shape=outs)(rate, value, start)


def spread_over(block, axis, count):
    copies = jnp.broadcast_to(block[None], (count,) + block.shape)
    return lax.all_to_all(copies, axis, 0, 0, tiled=True)


def carried_level(state, size):
    place = lax.axis_index(TM)
    every = spread_over(state, TM, size)
    level = jnp.ones_like(state[0]), jnp.zeros_like(state[1])
    for source in range(size - 1):
        joined = combine_maps(level, (every[source, 0], every[source, 1]))
        level = tuple(jnp.where(source < place, j, l) for j, l in zip(joined, level))
    return level[1]


def combine_maps(earlier, later):
    return (earlier[0] * later[0], later[0] * earlier[1] + later[1])


def gated(pre_values):
    split_at = pre_values.shape[1] // 2
    return jnp.tanh(pre_values[:, :split_at]) * jax.nn.sigmoid(pre_values[:, split_at:])


def gate_grad(pre_values, incoming_gradient):
    split_at = pre_values.shape[1] // 2
    tanh_part = jnp.tanh(pre_values[:, :split_at])
    gate_part = jax.nn.sigmoid(pre_values[:, split_at:])
    return jnp.concatenate(
        [
            incoming_gradient * gate_part * (1.0 - tanh_part * tanh_part),
            incoming_gradient * tanh_part * gate_part * (1.0 - gate_part),
        ],
        axis=1,
    )


def accumulate_with(operand, weights_block):
    return jnp.dot(operand, weights_block, preferred_element_type=jnp.float32)


def back_with(gradients, weights_block):
    return lax.dot_general(
        gradients, weights_block, (((1,), (1,)), ((), ())), preferred_element_type=jnp.float32
    )


def weight_term(operand, gradients):
    return lax.dot_general(
        operand, gradients, (((0,), (0,)), ((), ())), preferred_element_type=jnp.float32
    )


def on_device(frames, retention, first_conv, second_conv, cotangent):
    payload_elements = frames[0].astype(jnp.float32)
    keep_rate = retention[0]
    length, channels = payload_elements.shape
    short_lag = length // 4
    (local_last,) = drift(keep_rate, payload_elements, jnp.zeros((1, channels), jnp.float32), False)
    factor_last = jnp.prod(keep_rate, axis=0)
    state = jnp.stack([factor_last, local_last[0]])
    state, shards = lax.optimization_barrier((state, jnp.stack([first_conv, second_conv])))
    carried = carried_level(state, 16)
    both_full, carried = gather_weight(shards, carried)
    first_full, second_full = both_full[0], both_full[1]
    removed, _ = drift(keep_rate, payload_elements, carried[None, :], True)
    trend_removed = removed.astype(jnp.bfloat16)
    tail_rows = trend_removed[length - short_lag :]
    near_tail = passed_along(tail_rows, TM, 1)
    own_past = jnp.concatenate([near_tail, trend_removed[: length - short_lag]], axis=0)
    opening_layer_input = jnp.concatenate([own_past, trend_removed], axis=1)
    stacked_pre = accumulate_with(
        opening_layer_input, first_full
    )
    stacked_out = (trend_removed.astype(jnp.float32) + gated(stacked_pre)).astype(jnp.bfloat16)
    earlier_out = passed_along(stacked_out, TM, 1)
    closing_layer_input = jnp.concatenate([earlier_out, stacked_out], axis=1)
    second_pre = accumulate_with(
        closing_layer_input, second_full
    )
    top_hidden = (stacked_out.astype(jnp.float32) + gated(second_pre)).astype(jnp.bfloat16)
    incoming_gradient = cotangent[0].astype(jnp.float32)
    second_grad = gate_grad(second_pre, incoming_gradient).astype(jnp.bfloat16)
    second_cols = chip_half(weight_term(closing_layer_input, second_grad))
    closing_backward = back_with(
        second_grad, second_full
    )
    carried_back = passed_along(
        closing_backward[:, :channels].astype(jnp.bfloat16), TM, -1
    ).astype(jnp.float32)
    opening_upstream_gradient = incoming_gradient + closing_backward[:, channels:] + carried_back
    first_grad = gate_grad(stacked_pre, opening_upstream_gradient).astype(jnp.bfloat16)
    first_cols = chip_half(weight_term(opening_layer_input, first_grad))
    grads = reduce_gradient(jnp.stack([first_cols, second_cols]))
    grad_first, grad_second = grads[0], grads[1]
    return (top_hidden[None], grad_first, grad_second)


def solution(mesh):
    tm, fsdp = mesh.shape["tm"], mesh.shape["fsdp"]
    split = mesh.devices.reshape(tm // 2, 2, 4, fsdp // 8, 2)
    sub = Mesh(split, SUB_AXES)
    rows, frames = ("x", "y", "zh"), TM
    in_specs = (
        P(rows, frames, None),
        P(rows, frames, None),
        P(rows, None),
        P(rows, None),
        P(rows, frames, None),
    )
    out_specs = (P(rows, frames, None), P(rows, None), P(rows, None))
    return jax.shard_map(
        on_device, mesh=sub, in_specs=in_specs, out_specs=out_specs, check_vma=False
    )
```

```python
import jax
import jax.numpy as jnp
from jax import lax
from jax.experimental import pallas as pl
from jax.sharding import Mesh, PartitionSpec as P


def passed_along(value, axis, steps):
    count = 16
    leading, last = (max(0, -steps), min(count, count - steps))
    return lax.ppermute(value, axis, [(source, source + steps) for source in range(leading, last)])


TM = ("zl", "c")
SUB_AXES = ("zl", "c", "x", "y", "zh")


def rotated(value, axis, size, steps):
    return lax.ppermute(value, axis, [(i, (i + steps) % size) for i in range(size)])


def farthest_first(size):
    return sorted(range(1, size), key=lambda steps: -min(steps, size - steps))


def gather_over(block, axis, size, dim):
    place = lax.axis_index(axis)
    width = block.shape[dim]
    shape = list(block.shape)
    shape[dim] = width * size
    out = lax.dynamic_update_slice_in_dim(jnp.zeros(shape, block.dtype), block, place * width, dim)
    for steps in farthest_first(size):
        arrived = rotated(block, axis, size, steps)
        out = lax.dynamic_update_slice_in_dim(out, arrived, ((place - steps) % size) * width, dim)
    return out


def scatter_over(total, axis, size, dim):
    place = lax.axis_index(axis)
    width = total.shape[dim] // size
    sent = total.astype(jnp.bfloat16)
    acc = lax.dynamic_slice_in_dim(total, place * width, width, dim).astype(jnp.float32)
    for steps in farthest_first(size):
        piece = lax.dynamic_slice_in_dim(sent, ((place + steps) % size) * width, width, dim)
        acc = acc + rotated(piece, axis, size, steps).astype(jnp.float32)
    return acc


def summed_over(total, axis, size):
    stride = 1
    while stride < size:
        partner = lax.ppermute(total, axis, [(i, i ^ stride) for i in range(size)])
        total = total + partner
        stride *= 2
    return total


def halves(value, dim):
    half = value.shape[dim] // 2
    return lax.slice_in_dim(value, 0, half, axis=dim), lax.slice_in_dim(value, half, 2 * half, axis=dim)


def across_halves(value):
    pairs = [(zl * 2 + zh, (zl ^ 4) * 2 + 1 - zh) for zl in range(8) for zh in range(2)]
    return lax.ppermute(value, ("zl", "zh"), pairs)


def gather_halves(block, dim):
    other = across_halves(block)
    first = lax.axis_index("zh") == 0
    return jnp.concatenate([jnp.where(first, block, other), jnp.where(first, other, block)], axis=dim)


def scatter_halves(total, dim):
    keep, give = halves(total, dim)
    first = lax.axis_index("zh") == 0
    kept = jnp.where(first, keep, give).astype(jnp.float32)
    sent = jnp.where(first, give, keep).astype(jnp.bfloat16)
    return kept + across_halves(sent).astype(jnp.float32)


def crossed_pairs(steps, first):
    pairs = []
    for core in range(2):
        for x in range(4):
            for y in range(4):
                if (core == 0) == first:
                    target = (core, (x + steps) % 4, y)
                else:
                    target = (core, x, (y + steps) % 4)
                pairs.append((core * 16 + x * 4 + y, target[0] * 16 + target[1] * 4 + target[2]))
    return pairs


def crossed_place(first):
    core, x, y = lax.axis_index("c"), lax.axis_index("x"), lax.axis_index("y")
    return jnp.where((core == 0) == first, x, y)


def crossed_gather(block, first, dim):
    place = crossed_place(first)
    width = block.shape[dim]
    shape = list(block.shape)
    shape[dim] = width * 4
    out = lax.dynamic_update_slice_in_dim(jnp.zeros(shape, block.dtype), block, place * width, dim)
    for steps in farthest_first(4):
        arrived = lax.ppermute(block, ("c", "x", "y"), crossed_pairs(steps, first))
        out = lax.dynamic_update_slice_in_dim(out, arrived, ((place - steps) % 4) * width, dim)
    return out


def crossed_scatter(total, first, dim):
    place = crossed_place(first)
    width = total.shape[dim] // 4
    sent = total.astype(jnp.bfloat16)
    acc = lax.dynamic_slice_in_dim(total, place * width, width, dim).astype(jnp.float32)
    for steps in farthest_first(4):
        piece = lax.dynamic_slice_in_dim(sent, ((place + steps) % 4) * width, width, dim)
        arrived = lax.ppermute(piece, ("c", "x", "y"), crossed_pairs(steps, first))
        acc = acc + arrived.astype(jnp.float32)
    return acc


def core_order(blocks):
    swapped = jnp.swapaxes(blocks, 1, 2)
    return jnp.where(lax.axis_index("c") == 0, blocks, swapped)


def gather_weight(shard, ready):
    core = lax.axis_index("c")
    half = shard.shape[2] // 2
    mine = lax.dynamic_slice_in_dim(shard, core * half, half, 2)
    rows = gather_halves(mine, 1)
    count, block, width = rows.shape
    rows = crossed_gather(rows[:, None], False, 1)
    rows, ready = lax.optimization_barrier((rows, ready))
    rows = core_order(crossed_gather(rows[:, None], True, 1))
    rows = rows.reshape(count, 16 * block, width)
    return gather_over(rows, "c", 2, 2), ready


def chip_half(partial):
    return scatter_over(partial.astype(jnp.bfloat16), "c", 2, 1)


def reduce_gradient(cols):
    count, height, width = cols.shape
    blocks = core_order(cols.reshape(count, 4, 4, height // 16, width))
    blocks = crossed_scatter(crossed_scatter(blocks, True, 1), False, 2)
    rows = scatter_halves(blocks.reshape(count, height // 16, width), 1)
    total = summed_over(rows, "zl", 8)
    return gather_over(total, "c", 2, 2)


def drift_body(emit, rate_ref, value_ref, start_ref, *out_refs):
    rows = rate_ref.shape[0]

    def block(b, level):
        base = pl.multiple_of(b * 8, 8)
        rate = rate_ref[pl.ds(base, 8), :]
        value = value_ref[pl.ds(base, 8), :]
        for i in range(8):
            keep = rate[i : i + 1, :]
            level = keep * level + (1.0 - keep) * value[i : i + 1, :]
            if emit:
                out_refs[0][pl.ds(base + i, 1), :] = value[i : i + 1, :] - level
        return level

    out_refs[-1][...] = lax.fori_loop(0, rows // 8, block, start_ref[...])


def drift(rate, value, start, emit):
    rows, channels = rate.shape
    outs = [jax.ShapeDtypeStruct((1, channels), jnp.float32)]
    if emit:
        outs = [jax.ShapeDtypeStruct((rows, channels), jnp.float32)] + outs
    return pl.pallas_call(lambda *refs: drift_body(emit, *refs), out_shape=outs)(rate, value, start)


def spread_over(block, axis, count):
    copies = jnp.broadcast_to(block[None], (count,) + block.shape)
    return lax.all_to_all(copies, axis, 0, 0, tiled=True)


def carried_level(state, size):
    place = lax.axis_index(TM)
    every = spread_over(state, TM, size)
    level = jnp.ones_like(state[0]), jnp.zeros_like(state[1])
    for source in range(size - 1):
        joined = combine_maps(level, (every[source, 0], every[source, 1]))
        level = tuple(jnp.where(source < place, j, l) for j, l in zip(joined, level))
    return level[1]


def combine_maps(earlier, later):
    return (earlier[0] * later[0], later[0] * earlier[1] + later[1])


def gated(pre_values):
    split_at = pre_values.shape[1] // 2
    return jnp.tanh(pre_values[:, :split_at]) * jax.nn.sigmoid(pre_values[:, split_at:])


def gate_grad(pre_values, incoming_gradient):
    split_at = pre_values.shape[1] // 2
    tanh_part = jnp.tanh(pre_values[:, :split_at])
    gate_part = jax.nn.sigmoid(pre_values[:, split_at:])
    return jnp.concatenate(
        [
            incoming_gradient * gate_part * (1.0 - tanh_part * tanh_part),
            incoming_gradient * tanh_part * gate_part * (1.0 - gate_part),
        ],
        axis=1,
    )


def accumulate_with(operand, weights_block):
    return jnp.dot(operand, weights_block, preferred_element_type=jnp.float32)


def back_with(gradients, weights_block):
    return lax.dot_general(
        gradients, weights_block, (((1,), (1,)), ((), ())), preferred_element_type=jnp.float32
    )


def weight_term(operand, gradients):
    return lax.dot_general(
        operand, gradients, (((0,), (0,)), ((), ())), preferred_element_type=jnp.float32
    )


def on_device(frames, retention, first_conv, second_conv, cotangent):
    payload_elements = frames[0].astype(jnp.float32)
    keep_rate = retention[0]
    length, channels = payload_elements.shape
    short_lag = length // 4
    (local_last,) = drift(keep_rate, payload_elements, jnp.zeros((1, channels), jnp.float32), False)
    factor_last = jnp.prod(keep_rate, axis=0)
    state = jnp.stack([factor_last, local_last[0]])
    state, shards = lax.optimization_barrier((state, jnp.stack([first_conv, second_conv])))
    carried = carried_level(state, 16)
    both_full, carried = gather_weight(shards, carried)
    first_full, second_full = both_full[0], both_full[1]
    removed, _ = drift(keep_rate, payload_elements, carried[None, :], True)
    trend_removed = removed.astype(jnp.bfloat16)
    tail_rows = trend_removed[length - short_lag :]
    near_tail = passed_along(tail_rows, TM, 1)
    own_past = jnp.concatenate([near_tail, trend_removed[: length - short_lag]], axis=0)
    opening_layer_input = jnp.concatenate([own_past, trend_removed], axis=1)
    stacked_pre = accumulate_with(
        opening_layer_input, first_full
    )
    stacked_out = (trend_removed.astype(jnp.float32) + gated(stacked_pre)).astype(jnp.bfloat16)
    earlier_out = passed_along(stacked_out, TM, 1)
    closing_layer_input = jnp.concatenate([earlier_out, stacked_out], axis=1)
    second_pre = accumulate_with(
        closing_layer_input, second_full
    )
    top_hidden = (stacked_out.astype(jnp.float32) + gated(second_pre)).astype(jnp.bfloat16)
    incoming_gradient = cotangent[0].astype(jnp.float32)
    second_grad = gate_grad(second_pre, incoming_gradient).astype(jnp.bfloat16)
    second_cols = chip_half(weight_term(closing_layer_input, second_grad))
    closing_backward = back_with(
        second_grad, second_full
    )
    carried_back = passed_along(
        closing_backward[:, :channels].astype(jnp.bfloat16), TM, -1
    ).astype(jnp.float32)
    opening_upstream_gradient = incoming_gradient + closing_backward[:, channels:] + carried_back
    first_grad = gate_grad(stacked_pre, opening_upstream_gradient).astype(jnp.bfloat16)
    first_cols = chip_half(weight_term(opening_layer_input, first_grad))
    grads = reduce_gradient(jnp.stack([first_cols, second_cols]))
    grad_first, grad_second = grads[0], grads[1]
    return (top_hidden[None], grad_first, grad_second)


def solution(mesh):
    tm, fsdp = mesh.shape["tm"], mesh.shape["fsdp"]
    split = mesh.devices.reshape(tm // 2, 2, 4, fsdp // 8, 2)
    sub = Mesh(split, SUB_AXES)
    rows, frames = ("x", "y", "zh"), TM
    in_specs = (
        P(rows, frames, None),
        P(rows, frames, None),
        P(rows, None),
        P(rows, None),
        P(rows, frames, None),
    )
    out_specs = (P(rows, frames, None), P(rows, None), P(rows, None))
    return jax.shard_map(
        on_device, mesh=sub, in_specs=in_specs, out_specs=out_specs, check_vma=False
    )
```

```python
import jax
import jax.numpy as jnp
from jax import lax
from jax.experimental import pallas as pl
from jax.sharding import Mesh, PartitionSpec as P


def passed_along(value, axis, steps):
    count = 16
    leading, last = (max(0, -steps), min(count, count - steps))
    return lax.ppermute(value, axis, [(source, source + steps) for source in range(leading, last)])


TM = ("zl", "c")
SUB_AXES = ("zl", "c", "x", "y", "zh")


def rotated(value, axis, size, steps):
    return lax.ppermute(value, axis, [(i, (i + steps) % size) for i in range(size)])


def farthest_first(size):
    return sorted(range(1, size), key=lambda steps: -min(steps, size - steps))


def gather_over(block, axis, size, dim):
    place = lax.axis_index(axis)
    width = block.shape[dim]
    shape = list(block.shape)
    shape[dim] = width * size
    out = lax.dynamic_update_slice_in_dim(jnp.zeros(shape, block.dtype), block, place * width, dim)
    for steps in farthest_first(size):
        arrived = rotated(block, axis, size, steps)
        out = lax.dynamic_update_slice_in_dim(out, arrived, ((place - steps) % size) * width, dim)
    return out


def scatter_over(total, axis, size, dim):
    place = lax.axis_index(axis)
    width = total.shape[dim] // size
    sent = total.astype(jnp.bfloat16)
    acc = lax.dynamic_slice_in_dim(total, place * width, width, dim).astype(jnp.float32)
    for steps in farthest_first(size):
        piece = lax.dynamic_slice_in_dim(sent, ((place + steps) % size) * width, width, dim)
        acc = acc + rotated(piece, axis, size, steps).astype(jnp.float32)
    return acc


def summed_over(total, axis, size):
    stride = 1
    while stride < size:
        mine = total.astype(jnp.bfloat16)
        partner = lax.ppermute(mine, axis, [(i, i ^ stride) for i in range(size)])
        total = mine.astype(jnp.float32) + partner.astype(jnp.float32)
        stride *= 2
    return total


def halves(value, dim):
    half = value.shape[dim] // 2
    return lax.slice_in_dim(value, 0, half, axis=dim), lax.slice_in_dim(value, half, 2 * half, axis=dim)


def across_halves(value):
    pairs = [(zl * 2 + zh, (zl ^ 4) * 2 + 1 - zh) for zl in range(8) for zh in range(2)]
    return lax.ppermute(value, ("zl", "zh"), pairs)


def gather_halves(block, dim):
    other = across_halves(block)
    first = lax.axis_index("zh") == 0
    return jnp.concatenate([jnp.where(first, block, other), jnp.where(first, other, block)], axis=dim)


def scatter_halves(total, dim):
    keep, give = halves(total, dim)
    first = lax.axis_index("zh") == 0
    kept = jnp.where(first, keep, give).astype(jnp.float32)
    sent = jnp.where(first, give, keep).astype(jnp.bfloat16)
    return kept + across_halves(sent).astype(jnp.float32)


def crossed_pairs(steps, first):
    pairs = []
    for core in range(2):
        for x in range(4):
            for y in range(4):
                if (core == 0) == first:
                    target = (core, (x + steps) % 4, y)
                else:
                    target = (core, x, (y + steps) % 4)
                pairs.append((core * 16 + x * 4 + y, target[0] * 16 + target[1] * 4 + target[2]))
    return pairs


def crossed_place(first):
    core, x, y = lax.axis_index("c"), lax.axis_index("x"), lax.axis_index("y")
    return jnp.where((core == 0) == first, x, y)


def crossed_gather(block, first, dim):
    place = crossed_place(first)
    width = block.shape[dim]
    shape = list(block.shape)
    shape[dim] = width * 4
    out = lax.dynamic_update_slice_in_dim(jnp.zeros(shape, block.dtype), block, place * width, dim)
    for steps in farthest_first(4):
        arrived = lax.ppermute(block, ("c", "x", "y"), crossed_pairs(steps, first))
        out = lax.dynamic_update_slice_in_dim(out, arrived, ((place - steps) % 4) * width, dim)
    return out


def crossed_scatter(total, first, dim):
    place = crossed_place(first)
    width = total.shape[dim] // 4
    sent = total.astype(jnp.bfloat16)
    acc = lax.dynamic_slice_in_dim(total, place * width, width, dim).astype(jnp.float32)
    for steps in farthest_first(4):
        piece = lax.dynamic_slice_in_dim(sent, ((place + steps) % 4) * width, width, dim)
        arrived = lax.ppermute(piece, ("c", "x", "y"), crossed_pairs(steps, first))
        acc = acc + arrived.astype(jnp.float32)
    return acc


def core_order(blocks):
    swapped = jnp.swapaxes(blocks, 1, 2)
    return jnp.where(lax.axis_index("c") == 0, blocks, swapped)


def gather_weight(shard, ready):
    core = lax.axis_index("c")
    half = shard.shape[2] // 2
    mine = lax.dynamic_slice_in_dim(shard, core * half, half, 2)
    rows = gather_halves(mine, 1)
    count, block, width = rows.shape
    rows = crossed_gather(rows[:, None], False, 1)
    rows, ready = lax.optimization_barrier((rows, ready))
    rows = core_order(crossed_gather(rows[:, None], True, 1))
    rows = rows.reshape(count, 16 * block, width)
    return gather_over(rows, "c", 2, 2), ready


def chip_half(partial):
    return scatter_over(partial.astype(jnp.bfloat16), "c", 2, 1)


def reduce_gradient(cols):
    count, height, width = cols.shape
    blocks = core_order(cols.reshape(count, 4, 4, height // 16, width))
    blocks = crossed_scatter(crossed_scatter(blocks, True, 1), False, 2)
    rows = scatter_halves(blocks.reshape(count, height // 16, width), 1)
    total = summed_over(rows, "zl", 8)
    return gather_over(total, "c", 2, 2)


def drift_body(emit, rate_ref, value_ref, start_ref, *out_refs):
    rows = rate_ref.shape[0]

    def block(b, level):
        base = pl.multiple_of(b * 8, 8)
        rate = rate_ref[pl.ds(base, 8), :]
        value = value_ref[pl.ds(base, 8), :]
        for i in range(8):
            keep = rate[i : i + 1, :]
            level = keep * level + (1.0 - keep) * value[i : i + 1, :]
            if emit:
                out_refs[0][pl.ds(base + i, 1), :] = value[i : i + 1, :] - level
        return level

    out_refs[-1][...] = lax.fori_loop(0, rows // 8, block, start_ref[...])


def drift(rate, value, start, emit):
    rows, channels = rate.shape
    outs = [jax.ShapeDtypeStruct((1, channels), jnp.float32)]
    if emit:
        outs = [jax.ShapeDtypeStruct((rows, channels), jnp.float32)] + outs
    return pl.pallas_call(lambda *refs: drift_body(emit, *refs), out_shape=outs)(rate, value, start)


def spread_over(block, axis, count):
    copies = jnp.broadcast_to(block[None], (count,) + block.shape)
    return lax.all_to_all(copies, axis, 0, 0, tiled=True)


def carried_level(state, size):
    place = lax.axis_index(TM)
    every = spread_over(state, TM, size)
    level = jnp.ones_like(state[0]), jnp.zeros_like(state[1])
    for source in range(size - 1):
        joined = combine_maps(level, (every[source, 0], every[source, 1]))
        level = tuple(jnp.where(source < place, j, l) for j, l in zip(joined, level))
    return level[1]


def combine_maps(earlier, later):
    return (earlier[0] * later[0], later[0] * earlier[1] + later[1])


def gated(pre_values):
    split_at = pre_values.shape[1] // 2
    return jnp.tanh(pre_values[:, :split_at]) * jax.nn.sigmoid(pre_values[:, split_at:])


def gate_grad(pre_values, incoming_gradient):
    split_at = pre_values.shape[1] // 2
    tanh_part = jnp.tanh(pre_values[:, :split_at])
    gate_part = jax.nn.sigmoid(pre_values[:, split_at:])
    return jnp.concatenate(
        [
            incoming_gradient * gate_part * (1.0 - tanh_part * tanh_part),
            incoming_gradient * tanh_part * gate_part * (1.0 - gate_part),
        ],
        axis=1,
    )


def accumulate_with(operand, weights_block):
    return jnp.dot(operand, weights_block, preferred_element_type=jnp.float32)


def back_with(gradients, weights_block):
    return lax.dot_general(
        gradients, weights_block, (((1,), (1,)), ((), ())), preferred_element_type=jnp.float32
    )


def weight_term(operand, gradients):
    return lax.dot_general(
        operand, gradients, (((0,), (0,)), ((), ())), preferred_element_type=jnp.float32
    )


def on_device(frames, retention, first_conv, second_conv, cotangent):
    payload_elements = frames[0].astype(jnp.float32)
    keep_rate = retention[0]
    length, channels = payload_elements.shape
    short_lag = length // 4
    (local_last,) = drift(keep_rate, payload_elements, jnp.zeros((1, channels), jnp.float32), False)
    factor_last = jnp.prod(keep_rate, axis=0)
    state = jnp.stack([factor_last, local_last[0]])
    state, shards = lax.optimization_barrier((state, jnp.stack([first_conv, second_conv])))
    carried = carried_level(state, 16)
    both_full, carried = gather_weight(shards, carried)
    first_full, second_full = both_full[0], both_full[1]
    removed, _ = drift(keep_rate, payload_elements, carried[None, :], True)
    trend_removed = removed.astype(jnp.bfloat16)
    tail_rows = trend_removed[length - short_lag :]
    near_tail = passed_along(tail_rows, TM, 1)
    own_past = jnp.concatenate([near_tail, trend_removed[: length - short_lag]], axis=0)
    opening_layer_input = jnp.concatenate([own_past, trend_removed], axis=1)
    stacked_pre = accumulate_with(
        opening_layer_input, first_full
    )
    stacked_out = (trend_removed.astype(jnp.float32) + gated(stacked_pre)).astype(jnp.bfloat16)
    earlier_out = passed_along(stacked_out, TM, 1)
    closing_layer_input = jnp.concatenate([earlier_out, stacked_out], axis=1)
    second_pre = accumulate_with(
        closing_layer_input, second_full
    )
    top_hidden = (stacked_out.astype(jnp.float32) + gated(second_pre)).astype(jnp.bfloat16)
    incoming_gradient = cotangent[0].astype(jnp.float32)
    second_grad = gate_grad(second_pre, incoming_gradient).astype(jnp.bfloat16)
    second_cols = chip_half(weight_term(closing_layer_input, second_grad))
    closing_backward = back_with(
        second_grad, second_full
    )
    carried_back = passed_along(
        closing_backward[:, :channels].astype(jnp.bfloat16), TM, -1
    ).astype(jnp.float32)
    opening_upstream_gradient = incoming_gradient + closing_backward[:, channels:] + carried_back
    first_grad = gate_grad(stacked_pre, opening_upstream_gradient).astype(jnp.bfloat16)
    first_cols = chip_half(weight_term(opening_layer_input, first_grad))
    grads = reduce_gradient(jnp.stack([first_cols, second_cols]))
    grad_first, grad_second = grads[0], grads[1]
    return (top_hidden[None], grad_first, grad_second)


def solution(mesh):
    tm, fsdp = mesh.shape["tm"], mesh.shape["fsdp"]
    split = mesh.devices.reshape(tm // 2, 2, 4, fsdp // 8, 2)
    sub = Mesh(split, SUB_AXES)
    rows, frames = ("x", "y", "zh"), TM
    in_specs = (
        P(rows, frames, None),
        P(rows, frames, None),
        P(rows, None),
        P(rows, None),
        P(rows, frames, None),
    )
    out_specs = (P(rows, frames, None), P(rows, None), P(rows, None))
    return jax.shard_map(
        on_device, mesh=sub, in_specs=in_specs, out_specs=out_specs, check_vma=False
    )
```

```python
import jax
import jax.numpy as jnp
from jax import lax
from jax.experimental import pallas as pl
from jax.sharding import Mesh, PartitionSpec as P


def passed_along(value, axis, steps):
    count = 16
    leading, last = (max(0, -steps), min(count, count - steps))
    return lax.ppermute(value, axis, [(source, source + steps) for source in range(leading, last)])


TM = ("zl", "c")
SUB_AXES = ("zl", "c", "x", "y", "zh")


def rotated(value, axis, size, steps):
    return lax.ppermute(value, axis, [(i, (i + steps) % size) for i in range(size)])


def farthest_first(size):
    return sorted(range(1, size), key=lambda steps: -min(steps, size - steps))


def gather_over(block, axis, size, dim):
    place = lax.axis_index(axis)
    width = block.shape[dim]
    shape = list(block.shape)
    shape[dim] = width * size
    out = lax.dynamic_update_slice_in_dim(jnp.zeros(shape, block.dtype), block, place * width, dim)
    for steps in farthest_first(size):
        arrived = rotated(block, axis, size, steps)
        out = lax.dynamic_update_slice_in_dim(out, arrived, ((place - steps) % size) * width, dim)
    return out


def scatter_over(total, axis, size, dim):
    place = lax.axis_index(axis)
    width = total.shape[dim] // size
    sent = total.astype(jnp.bfloat16)
    acc = lax.dynamic_slice_in_dim(total, place * width, width, dim).astype(jnp.float32)
    for steps in farthest_first(size):
        piece = lax.dynamic_slice_in_dim(sent, ((place + steps) % size) * width, width, dim)
        acc = acc + rotated(piece, axis, size, steps).astype(jnp.float32)
    return acc


def summed_over(total, axis, size):
    stride = 1
    while stride < size:
        mine = total.astype(jnp.bfloat16)
        partner = lax.ppermute(mine, axis, [(i, i ^ stride) for i in range(size)])
        total = mine.astype(jnp.float32) + partner.astype(jnp.float32)
        stride *= 2
    return total


def halves(value, dim):
    half = value.shape[dim] // 2
    return lax.slice_in_dim(value, 0, half, axis=dim), lax.slice_in_dim(value, half, 2 * half, axis=dim)


def across_halves(value):
    pairs = [(zl * 2 + zh, (zl ^ 4) * 2 + 1 - zh) for zl in range(8) for zh in range(2)]
    return lax.ppermute(value, ("zl", "zh"), pairs)


def gather_halves(block, dim):
    other = across_halves(block)
    first = lax.axis_index("zh") == 0
    return jnp.concatenate([jnp.where(first, block, other), jnp.where(first, other, block)], axis=dim)


def scatter_halves(total, dim):
    keep, give = halves(total, dim)
    first = lax.axis_index("zh") == 0
    kept = jnp.where(first, keep, give).astype(jnp.float32)
    sent = jnp.where(first, give, keep).astype(jnp.bfloat16)
    return kept + across_halves(sent).astype(jnp.float32)


def crossed_pairs(steps, first):
    pairs = []
    for core in range(2):
        for x in range(4):
            for y in range(4):
                if (core == 0) == first:
                    target = (core, (x + steps) % 4, y)
                else:
                    target = (core, x, (y + steps) % 4)
                pairs.append((core * 16 + x * 4 + y, target[0] * 16 + target[1] * 4 + target[2]))
    return pairs


def crossed_place(first):
    core, x, y = lax.axis_index("c"), lax.axis_index("x"), lax.axis_index("y")
    return jnp.where((core == 0) == first, x, y)


def crossed_gather(block, first, dim):
    place = crossed_place(first)
    width = block.shape[dim]
    shape = list(block.shape)
    shape[dim] = width * 4
    out = lax.dynamic_update_slice_in_dim(jnp.zeros(shape, block.dtype), block, place * width, dim)
    for steps in farthest_first(4):
        arrived = lax.ppermute(block, ("c", "x", "y"), crossed_pairs(steps, first))
        out = lax.dynamic_update_slice_in_dim(out, arrived, ((place - steps) % 4) * width, dim)
    return out


def crossed_scatter(total, first, dim):
    place = crossed_place(first)
    width = total.shape[dim] // 4
    sent = total.astype(jnp.bfloat16)
    acc = lax.dynamic_slice_in_dim(total, place * width, width, dim).astype(jnp.float32)
    for steps in farthest_first(4):
        piece = lax.dynamic_slice_in_dim(sent, ((place + steps) % 4) * width, width, dim)
        arrived = lax.ppermute(piece, ("c", "x", "y"), crossed_pairs(steps, first))
        acc = acc + arrived.astype(jnp.float32)
    return acc


def core_order(blocks):
    swapped = jnp.swapaxes(blocks, 1, 2)
    return jnp.where(lax.axis_index("c") == 0, blocks, swapped)


def gather_weight(shard, ready, after):
    core = lax.axis_index("c")
    half = shard.shape[2] // 2
    mine = lax.dynamic_slice_in_dim(shard, core * half, half, 2)
    rows = gather_halves(mine, 1)
    count, block, width = rows.shape
    rows = crossed_gather(rows[:, None], False, 1)
    rows, ready = lax.optimization_barrier((rows, ready))
    rows = core_order(crossed_gather(rows[:, None], True, 1))
    rows, done = lax.optimization_barrier((rows, after(ready)))
    rows = rows.reshape(count, 16 * block, width)
    return gather_over(rows, "c", 2, 2), done


def chip_half(partial):
    return scatter_over(partial.astype(jnp.bfloat16), "c", 2, 1)


def reduce_gradient(cols):
    count, height, width = cols.shape
    blocks = core_order(cols.reshape(count, 4, 4, height // 16, width))
    blocks = crossed_scatter(crossed_scatter(blocks, True, 1), False, 2)
    rows = scatter_halves(blocks.reshape(count, height // 16, width), 1)
    total = summed_over(rows, "zl", 8)
    return gather_over(total, "c", 2, 2)


def drift_body(emit, rate_ref, value_ref, start_ref, *out_refs):
    rows = rate_ref.shape[0]

    def block(b, level):
        base = pl.multiple_of(b * 8, 8)
        rate = rate_ref[pl.ds(base, 8), :]
        value = value_ref[pl.ds(base, 8), :]
        for i in range(8):
            keep = rate[i : i + 1, :]
            level = keep * level + (1.0 - keep) * value[i : i + 1, :]
            if emit:
                out_refs[0][pl.ds(base + i, 1), :] = value[i : i + 1, :] - level
        return level

    out_refs[-1][...] = lax.fori_loop(0, rows // 8, block, start_ref[...])


def drift(rate, value, start, emit):
    rows, channels = rate.shape
    outs = [jax.ShapeDtypeStruct((1, channels), jnp.float32)]
    if emit:
        outs = [jax.ShapeDtypeStruct((rows, channels), jnp.float32)] + outs
    return pl.pallas_call(lambda *refs: drift_body(emit, *refs), out_shape=outs)(rate, value, start)


def spread_over(block, axis, count):
    copies = jnp.broadcast_to(block[None], (count,) + block.shape)
    return lax.all_to_all(copies, axis, 0, 0, tiled=True)


def carried_level(state, size):
    place = lax.axis_index(TM)
    every = spread_over(state, TM, size)
    level = jnp.ones_like(state[0]), jnp.zeros_like(state[1])
    for source in range(size - 1):
        joined = combine_maps(level, (every[source, 0], every[source, 1]))
        level = tuple(jnp.where(source < place, j, l) for j, l in zip(joined, level))
    return level[1]


def combine_maps(earlier, later):
    return (earlier[0] * later[0], later[0] * earlier[1] + later[1])


def gated(pre_values):
    split_at = pre_values.shape[1] // 2
    return jnp.tanh(pre_values[:, :split_at]) * jax.nn.sigmoid(pre_values[:, split_at:])


def gate_grad(pre_values, incoming_gradient):
    split_at = pre_values.shape[1] // 2
    tanh_part = jnp.tanh(pre_values[:, :split_at])
    gate_part = jax.nn.sigmoid(pre_values[:, split_at:])
    return jnp.concatenate(
        [
            incoming_gradient * gate_part * (1.0 - tanh_part * tanh_part),
            incoming_gradient * tanh_part * gate_part * (1.0 - gate_part),
        ],
        axis=1,
    )


def accumulate_with(operand, weights_block):
    return jnp.dot(operand, weights_block, preferred_element_type=jnp.float32)


def back_with(gradients, weights_block):
    return lax.dot_general(
        gradients, weights_block, (((1,), (1,)), ((), ())), preferred_element_type=jnp.float32
    )


def weight_term(operand, gradients):
    return lax.dot_general(
        operand, gradients, (((0,), (0,)), ((), ())), preferred_element_type=jnp.float32
    )


def on_device(frames, retention, first_conv, second_conv, cotangent):
    payload_elements = frames[0].astype(jnp.float32)
    keep_rate = retention[0]
    length, channels = payload_elements.shape
    short_lag = length // 4
    (local_last,) = drift(keep_rate, payload_elements, jnp.zeros((1, channels), jnp.float32), False)
    factor_last = jnp.prod(keep_rate, axis=0)
    state = jnp.stack([factor_last, local_last[0]])
    state, shards = lax.optimization_barrier((state, jnp.stack([first_conv, second_conv])))
    carried = carried_level(state, 16)
    both_full, removed = gather_weight(
        shards, carried, lambda level: drift(keep_rate, payload_elements, level[None, :], True)[0]
    )
    first_full, second_full = both_full[0], both_full[1]
    trend_removed = removed.astype(jnp.bfloat16)
    tail_rows = trend_removed[length - short_lag :]
    near_tail = passed_along(tail_rows, TM, 1)
    own_past = jnp.concatenate([near_tail, trend_removed[: length - short_lag]], axis=0)
    opening_layer_input = jnp.concatenate([own_past, trend_removed], axis=1)
    stacked_pre = accumulate_with(
        opening_layer_input, first_full
    )
    stacked_out = (trend_removed.astype(jnp.float32) + gated(stacked_pre)).astype(jnp.bfloat16)
    earlier_out = passed_along(stacked_out, TM, 1)
    closing_layer_input = jnp.concatenate([earlier_out, stacked_out], axis=1)
    second_pre = accumulate_with(
        closing_layer_input, second_full
    )
    top_hidden = (stacked_out.astype(jnp.float32) + gated(second_pre)).astype(jnp.bfloat16)
    incoming_gradient = cotangent[0].astype(jnp.float32)
    second_grad = gate_grad(second_pre, incoming_gradient).astype(jnp.bfloat16)
    second_cols = chip_half(weight_term(closing_layer_input, second_grad))
    closing_backward = back_with(
        second_grad, second_full
    )
    carried_back = passed_along(
        closing_backward[:, :channels].astype(jnp.bfloat16), TM, -1
    ).astype(jnp.float32)
    opening_upstream_gradient = incoming_gradient + closing_backward[:, channels:] + carried_back
    first_grad = gate_grad(stacked_pre, opening_upstream_gradient).astype(jnp.bfloat16)
    first_cols = chip_half(weight_term(opening_layer_input, first_grad))
    grads = reduce_gradient(jnp.stack([first_cols, second_cols]))
    grad_first, grad_second = grads[0], grads[1]
    return (top_hidden[None], grad_first, grad_second)


def solution(mesh):
    tm, fsdp = mesh.shape["tm"], mesh.shape["fsdp"]
    split = mesh.devices.reshape(tm // 2, 2, 4, fsdp // 8, 2)
    sub = Mesh(split, SUB_AXES)
    rows, frames = ("x", "y", "zh"), TM
    in_specs = (
        P(rows, frames, None),
        P(rows, frames, None),
        P(rows, None),
        P(rows, None),
        P(rows, frames, None),
    )
    out_specs = (P(rows, frames, None), P(rows, None), P(rows, None))
    return jax.shard_map(
        on_device, mesh=sub, in_specs=in_specs, out_specs=out_specs, check_vma=False
    )
```

```python
import jax
import jax.numpy as jnp
from jax import lax
from jax.experimental import pallas as pl
from jax.sharding import Mesh, PartitionSpec as P


def passed_along(value, axis, steps):
    count = 16
    leading, last = (max(0, -steps), min(count, count - steps))
    return lax.ppermute(value, axis, [(source, source + steps) for source in range(leading, last)])


TM = ("zl", "c")
SUB_AXES = ("zl", "c", "x", "y", "zh")


def rotated(value, axis, size, steps):
    return lax.ppermute(value, axis, [(i, (i + steps) % size) for i in range(size)])


def farthest_first(size):
    return sorted(range(1, size), key=lambda steps: -min(steps, size - steps))


def gather_over(block, axis, size, dim):
    place = lax.axis_index(axis)
    width = block.shape[dim]
    shape = list(block.shape)
    shape[dim] = width * size
    out = lax.dynamic_update_slice_in_dim(jnp.zeros(shape, block.dtype), block, place * width, dim)
    for steps in farthest_first(size):
        arrived = rotated(block, axis, size, steps)
        out = lax.dynamic_update_slice_in_dim(out, arrived, ((place - steps) % size) * width, dim)
    return out


def scatter_over(total, axis, size, dim):
    place = lax.axis_index(axis)
    width = total.shape[dim] // size
    sent = total.astype(jnp.bfloat16)
    acc = lax.dynamic_slice_in_dim(total, place * width, width, dim).astype(jnp.float32)
    for steps in farthest_first(size):
        piece = lax.dynamic_slice_in_dim(sent, ((place + steps) % size) * width, width, dim)
        acc = acc + rotated(piece, axis, size, steps).astype(jnp.float32)
    return acc


def summed_over(total, axis, size):
    stride = 1
    while stride < size:
        mine = total.astype(jnp.bfloat16)
        partner = lax.ppermute(mine, axis, [(i, i ^ stride) for i in range(size)])
        total = mine.astype(jnp.float32) + partner.astype(jnp.float32)
        stride *= 2
    return total


def halves(value, dim):
    half = value.shape[dim] // 2
    return lax.slice_in_dim(value, 0, half, axis=dim), lax.slice_in_dim(value, half, 2 * half, axis=dim)


def across_halves(value):
    pairs = [(zl * 2 + zh, (zl ^ 4) * 2 + 1 - zh) for zl in range(8) for zh in range(2)]
    return lax.ppermute(value, ("zl", "zh"), pairs)


def gather_halves(block, dim):
    other = across_halves(block)
    first = lax.axis_index("zh") == 0
    return jnp.concatenate([jnp.where(first, block, other), jnp.where(first, other, block)], axis=dim)


def scatter_halves(total, dim):
    keep, give = halves(total, dim)
    first = lax.axis_index("zh") == 0
    kept = jnp.where(first, keep, give).astype(jnp.float32)
    sent = jnp.where(first, give, keep).astype(jnp.bfloat16)
    return kept + across_halves(sent).astype(jnp.float32)


def crossed_pairs(steps, first):
    pairs = []
    for core in range(2):
        for x in range(4):
            for y in range(4):
                if (core == 0) == first:
                    target = (core, (x + steps) % 4, y)
                else:
                    target = (core, x, (y + steps) % 4)
                pairs.append((core * 16 + x * 4 + y, target[0] * 16 + target[1] * 4 + target[2]))
    return pairs


def crossed_place(first):
    core, x, y = lax.axis_index("c"), lax.axis_index("x"), lax.axis_index("y")
    return jnp.where((core == 0) == first, x, y)


def crossed_gather(block, first, dim):
    place = crossed_place(first)
    width = block.shape[dim]
    shape = list(block.shape)
    shape[dim] = width * 4
    out = lax.dynamic_update_slice_in_dim(jnp.zeros(shape, block.dtype), block, place * width, dim)
    for steps in farthest_first(4):
        arrived = lax.ppermute(block, ("c", "x", "y"), crossed_pairs(steps, first))
        out = lax.dynamic_update_slice_in_dim(out, arrived, ((place - steps) % 4) * width, dim)
    return out


def crossed_scatter(total, first, dim):
    place = crossed_place(first)
    width = total.shape[dim] // 4
    sent = total.astype(jnp.bfloat16)
    acc = lax.dynamic_slice_in_dim(total, place * width, width, dim).astype(jnp.float32)
    for steps in farthest_first(4):
        piece = lax.dynamic_slice_in_dim(sent, ((place + steps) % 4) * width, width, dim)
        arrived = lax.ppermute(piece, ("c", "x", "y"), crossed_pairs(steps, first))
        acc = acc + arrived.astype(jnp.float32)
    return acc


def core_order(blocks):
    swapped = jnp.swapaxes(blocks, 1, 2)
    return jnp.where(lax.axis_index("c") == 0, blocks, swapped)


def gather_weight(shard, state, after):
    core = lax.axis_index("c")
    half = shard.shape[2] // 2
    mine = lax.dynamic_slice_in_dim(shard, core * half, half, 2)
    rows = gather_halves(mine, 1)
    rows, state = lax.optimization_barrier((rows, state))
    ready = carried_level(state, 16)
    count, block, width = rows.shape
    rows = crossed_gather(rows[:, None], False, 1)
    rows, ready = lax.optimization_barrier((rows, ready))
    rows = core_order(crossed_gather(rows[:, None], True, 1))
    rows, done = lax.optimization_barrier((rows, after(ready)))
    rows = rows.reshape(count, 16 * block, width)
    return gather_over(rows, "c", 2, 2), done


def chip_half(partial):
    return scatter_over(partial.astype(jnp.bfloat16), "c", 2, 1)


def reduce_gradient(cols):
    count, height, width = cols.shape
    blocks = core_order(cols.reshape(count, 4, 4, height // 16, width))
    blocks = crossed_scatter(crossed_scatter(blocks, True, 1), False, 2)
    rows = scatter_halves(blocks.reshape(count, height // 16, width), 1)
    total = summed_over(rows, "zl", 8)
    return gather_over(total, "c", 2, 2)


def drift_body(emit, rate_ref, value_ref, start_ref, *out_refs):
    rows = rate_ref.shape[0]

    def block(b, level):
        base = pl.multiple_of(b * 8, 8)
        rate = rate_ref[pl.ds(base, 8), :]
        value = value_ref[pl.ds(base, 8), :]
        for i in range(8):
            keep = rate[i : i + 1, :]
            level = keep * level + (1.0 - keep) * value[i : i + 1, :]
            if emit:
                out_refs[0][pl.ds(base + i, 1), :] = value[i : i + 1, :] - level
        return level

    out_refs[-1][...] = lax.fori_loop(0, rows // 8, block, start_ref[...])


def drift(rate, value, start, emit):
    rows, channels = rate.shape
    outs = [jax.ShapeDtypeStruct((1, channels), jnp.float32)]
    if emit:
        outs = [jax.ShapeDtypeStruct((rows, channels), jnp.float32)] + outs
    return pl.pallas_call(lambda *refs: drift_body(emit, *refs), out_shape=outs)(rate, value, start)


def spread_over(block, axis, count):
    copies = jnp.broadcast_to(block[None], (count,) + block.shape)
    return lax.all_to_all(copies, axis, 0, 0, tiled=True)


def carried_level(state, size):
    place = lax.axis_index(TM)
    every = spread_over(state, TM, size)
    level = jnp.ones_like(state[0]), jnp.zeros_like(state[1])
    for source in range(size - 1):
        joined = combine_maps(level, (every[source, 0], every[source, 1]))
        level = tuple(jnp.where(source < place, j, l) for j, l in zip(joined, level))
    return level[1]


def combine_maps(earlier, later):
    return (earlier[0] * later[0], later[0] * earlier[1] + later[1])


def gated(pre_values):
    split_at = pre_values.shape[1] // 2
    return jnp.tanh(pre_values[:, :split_at]) * jax.nn.sigmoid(pre_values[:, split_at:])


def gate_grad(pre_values, incoming_gradient):
    split_at = pre_values.shape[1] // 2
    tanh_part = jnp.tanh(pre_values[:, :split_at])
    gate_part = jax.nn.sigmoid(pre_values[:, split_at:])
    return jnp.concatenate(
        [
            incoming_gradient * gate_part * (1.0 - tanh_part * tanh_part),
            incoming_gradient * tanh_part * gate_part * (1.0 - gate_part),
        ],
        axis=1,
    )


def accumulate_with(operand, weights_block):
    return jnp.dot(operand, weights_block, preferred_element_type=jnp.float32)


def back_with(gradients, weights_block):
    return lax.dot_general(
        gradients, weights_block, (((1,), (1,)), ((), ())), preferred_element_type=jnp.float32
    )


def weight_term(operand, gradients):
    return lax.dot_general(
        operand, gradients, (((0,), (0,)), ((), ())), preferred_element_type=jnp.float32
    )


def on_device(frames, retention, first_conv, second_conv, cotangent):
    payload_elements = frames[0].astype(jnp.float32)
    keep_rate = retention[0]
    length, channels = payload_elements.shape
    short_lag = length // 4
    (local_last,) = drift(keep_rate, payload_elements, jnp.zeros((1, channels), jnp.float32), False)
    factor_last = jnp.prod(keep_rate, axis=0)
    state = jnp.stack([factor_last, local_last[0]])
    both_full, removed = gather_weight(
        jnp.stack([first_conv, second_conv]), state, lambda level: drift(keep_rate, payload_elements, level[None, :], True)[0]
    )
    first_full, second_full = both_full[0], both_full[1]
    trend_removed = removed.astype(jnp.bfloat16)
    tail_rows = trend_removed[length - short_lag :]
    near_tail = passed_along(tail_rows, TM, 1)
    own_past = jnp.concatenate([near_tail, trend_removed[: length - short_lag]], axis=0)
    opening_layer_input = jnp.concatenate([own_past, trend_removed], axis=1)
    stacked_pre = accumulate_with(
        opening_layer_input, first_full
    )
    stacked_out = (trend_removed.astype(jnp.float32) + gated(stacked_pre)).astype(jnp.bfloat16)
    earlier_out = passed_along(stacked_out, TM, 1)
    closing_layer_input = jnp.concatenate([earlier_out, stacked_out], axis=1)
    second_pre = accumulate_with(
        closing_layer_input, second_full
    )
    top_hidden = (stacked_out.astype(jnp.float32) + gated(second_pre)).astype(jnp.bfloat16)
    incoming_gradient = cotangent[0].astype(jnp.float32)
    second_grad = gate_grad(second_pre, incoming_gradient).astype(jnp.bfloat16)
    second_cols = chip_half(weight_term(closing_layer_input, second_grad))
    closing_backward = back_with(
        second_grad, second_full
    )
    carried_back = passed_along(
        closing_backward[:, :channels].astype(jnp.bfloat16), TM, -1
    ).astype(jnp.float32)
    opening_upstream_gradient = incoming_gradient + closing_backward[:, channels:] + carried_back
    first_grad = gate_grad(stacked_pre, opening_upstream_gradient).astype(jnp.bfloat16)
    first_cols = chip_half(weight_term(opening_layer_input, first_grad))
    grads = reduce_gradient(jnp.stack([first_cols, second_cols]))
    grad_first, grad_second = grads[0], grads[1]
    return (top_hidden[None], grad_first, grad_second)


def solution(mesh):
    tm, fsdp = mesh.shape["tm"], mesh.shape["fsdp"]
    split = mesh.devices.reshape(tm // 2, 2, 4, fsdp // 8, 2)
    sub = Mesh(split, SUB_AXES)
    rows, frames = ("x", "y", "zh"), TM
    in_specs = (
        P(rows, frames, None),
        P(rows, frames, None),
        P(rows, None),
        P(rows, None),
        P(rows, frames, None),
    )
    out_specs = (P(rows, frames, None), P(rows, None), P(rows, None))
    return jax.shard_map(
        on_device, mesh=sub, in_specs=in_specs, out_specs=out_specs, check_vma=False
    )
```

```python
import jax
import jax.numpy as jnp
from jax import lax
from jax.experimental import pallas as pl
from jax.sharding import Mesh, PartitionSpec as P


def passed_along(value, axis, steps):
    count = 16
    leading, last = (max(0, -steps), min(count, count - steps))
    return lax.ppermute(value, axis, [(source, source + steps) for source in range(leading, last)])


TM = ("zl", "c")
SUB_AXES = ("zl", "c", "x", "y", "zh")


def rotated(value, axis, size, steps):
    return lax.ppermute(value, axis, [(i, (i + steps) % size) for i in range(size)])


def farthest_first(size):
    return sorted(range(1, size), key=lambda steps: -min(steps, size - steps))


def gather_over(block, axis, size, dim):
    place = lax.axis_index(axis)
    width = block.shape[dim]
    shape = list(block.shape)
    shape[dim] = width * size
    out = lax.dynamic_update_slice_in_dim(jnp.zeros(shape, block.dtype), block, place * width, dim)
    for steps in farthest_first(size):
        arrived = rotated(block, axis, size, steps)
        out = lax.dynamic_update_slice_in_dim(out, arrived, ((place - steps) % size) * width, dim)
    return out


def scatter_over(total, axis, size, dim):
    place = lax.axis_index(axis)
    width = total.shape[dim] // size
    sent = total.astype(jnp.bfloat16)
    acc = lax.dynamic_slice_in_dim(total, place * width, width, dim).astype(jnp.float32)
    for steps in farthest_first(size):
        piece = lax.dynamic_slice_in_dim(sent, ((place + steps) % size) * width, width, dim)
        acc = acc + rotated(piece, axis, size, steps).astype(jnp.float32)
    return acc


def summed_over(total, axis, size):
    stride = 1
    while stride < size:
        mine = total.astype(jnp.bfloat16)
        partner = lax.ppermute(mine, axis, [(i, i ^ stride) for i in range(size)])
        total = mine.astype(jnp.float32) + partner.astype(jnp.float32)
        stride *= 2
    return total


def halves(value, dim):
    half = value.shape[dim] // 2
    return lax.slice_in_dim(value, 0, half, axis=dim), lax.slice_in_dim(value, half, 2 * half, axis=dim)


def across_halves(value):
    pairs = [(zl * 2 + zh, (zl ^ 4) * 2 + 1 - zh) for zl in range(8) for zh in range(2)]
    return lax.ppermute(value, ("zl", "zh"), pairs)


def gather_halves(block, dim):
    other = across_halves(block)
    first = lax.axis_index("zh") == 0
    return jnp.concatenate([jnp.where(first, block, other), jnp.where(first, other, block)], axis=dim)


def scatter_halves(total, dim):
    keep, give = halves(total, dim)
    first = lax.axis_index("zh") == 0
    kept = jnp.where(first, keep, give).astype(jnp.float32)
    sent = jnp.where(first, give, keep).astype(jnp.bfloat16)
    return kept + across_halves(sent).astype(jnp.float32)


def crossed_pairs(steps, first):
    pairs = []
    for core in range(2):
        for x in range(4):
            for y in range(4):
                if (core == 0) == first:
                    target = (core, (x + steps) % 4, y)
                else:
                    target = (core, x, (y + steps) % 4)
                pairs.append((core * 16 + x * 4 + y, target[0] * 16 + target[1] * 4 + target[2]))
    return pairs


def crossed_place(first):
    core, x, y = lax.axis_index("c"), lax.axis_index("x"), lax.axis_index("y")
    return jnp.where((core == 0) == first, x, y)


def crossed_gather(block, first, dim):
    place = crossed_place(first)
    width = block.shape[dim]
    shape = list(block.shape)
    shape[dim] = width * 4
    out = lax.dynamic_update_slice_in_dim(jnp.zeros(shape, block.dtype), block, place * width, dim)
    for steps in farthest_first(4):
        arrived = lax.ppermute(block, ("c", "x", "y"), crossed_pairs(steps, first))
        out = lax.dynamic_update_slice_in_dim(out, arrived, ((place - steps) % 4) * width, dim)
    return out


def crossed_scatter(total, first, dim):
    place = crossed_place(first)
    width = total.shape[dim] // 4
    sent = total.astype(jnp.bfloat16)
    acc = lax.dynamic_slice_in_dim(total, place * width, width, dim).astype(jnp.float32)
    for steps in farthest_first(4):
        piece = lax.dynamic_slice_in_dim(sent, ((place + steps) % 4) * width, width, dim)
        arrived = lax.ppermute(piece, ("c", "x", "y"), crossed_pairs(steps, first))
        acc = acc + arrived.astype(jnp.float32)
    return acc


def core_order(blocks):
    swapped = jnp.swapaxes(blocks, 1, 2)
    return jnp.where(lax.axis_index("c") == 0, blocks, swapped)


def gather_weight(shard, state, after):
    core = lax.axis_index("c")
    half = shard.shape[2] // 2
    mine = lax.dynamic_slice_in_dim(shard, core * half, half, 2)
    rows = gather_halves(mine, 1)
    ready = carried_level(state, 16)
    rows, _ = lax.optimization_barrier((rows, state))
    count, block, width = rows.shape
    rows = crossed_gather(rows[:, None], False, 1)
    rows, ready = lax.optimization_barrier((rows, ready))
    rows = core_order(crossed_gather(rows[:, None], True, 1))
    rows, done = lax.optimization_barrier((rows, after(ready)))
    rows = rows.reshape(count, 16 * block, width)
    return gather_over(rows, "c", 2, 2), done


def chip_half(partial):
    return scatter_over(partial.astype(jnp.bfloat16), "c", 2, 1)


def reduce_gradient(cols):
    count, height, width = cols.shape
    blocks = core_order(cols.reshape(count, 4, 4, height // 16, width))
    blocks = crossed_scatter(crossed_scatter(blocks, True, 1), False, 2)
    rows = scatter_halves(blocks.reshape(count, height // 16, width), 1)
    total = summed_over(rows, "zl", 8)
    return gather_over(total, "c", 2, 2)


def drift_body(emit, rate_ref, value_ref, start_ref, *out_refs):
    rows = rate_ref.shape[0]

    def block(b, level):
        base = pl.multiple_of(b * 8, 8)
        rate = rate_ref[pl.ds(base, 8), :]
        value = value_ref[pl.ds(base, 8), :]
        for i in range(8):
            keep = rate[i : i + 1, :]
            level = keep * level + (1.0 - keep) * value[i : i + 1, :]
            if emit:
                out_refs[0][pl.ds(base + i, 1), :] = value[i : i + 1, :] - level
        return level

    out_refs[-1][...] = lax.fori_loop(0, rows // 8, block, start_ref[...])


def drift(rate, value, start, emit):
    rows, channels = rate.shape
    outs = [jax.ShapeDtypeStruct((1, channels), jnp.float32)]
    if emit:
        outs = [jax.ShapeDtypeStruct((rows, channels), jnp.float32)] + outs
    return pl.pallas_call(lambda *refs: drift_body(emit, *refs), out_shape=outs)(rate, value, start)


def spread_over(block, axis, count):
    copies = jnp.broadcast_to(block[None], (count,) + block.shape)
    return lax.all_to_all(copies, axis, 0, 0, tiled=True)


def carried_level(state, size):
    place = lax.axis_index(TM)
    every = spread_over(state, TM, size)
    level = jnp.ones_like(state[0]), jnp.zeros_like(state[1])
    for source in range(size - 1):
        joined = combine_maps(level, (every[source, 0], every[source, 1]))
        level = tuple(jnp.where(source < place, j, l) for j, l in zip(joined, level))
    return level[1]


def combine_maps(earlier, later):
    return (earlier[0] * later[0], later[0] * earlier[1] + later[1])


def gated(pre_values):
    split_at = pre_values.shape[1] // 2
    return jnp.tanh(pre_values[:, :split_at]) * jax.nn.sigmoid(pre_values[:, split_at:])


def gate_grad(pre_values, incoming_gradient):
    split_at = pre_values.shape[1] // 2
    tanh_part = jnp.tanh(pre_values[:, :split_at])
    gate_part = jax.nn.sigmoid(pre_values[:, split_at:])
    return jnp.concatenate(
        [
            incoming_gradient * gate_part * (1.0 - tanh_part * tanh_part),
            incoming_gradient * tanh_part * gate_part * (1.0 - gate_part),
        ],
        axis=1,
    )


def accumulate_with(operand, weights_block):
    return jnp.dot(operand, weights_block, preferred_element_type=jnp.float32)


def back_with(gradients, weights_block):
    return lax.dot_general(
        gradients, weights_block, (((1,), (1,)), ((), ())), preferred_element_type=jnp.float32
    )


def weight_term(operand, gradients):
    return lax.dot_general(
        operand, gradients, (((0,), (0,)), ((), ())), preferred_element_type=jnp.float32
    )


def on_device(frames, retention, first_conv, second_conv, cotangent):
    payload_elements = frames[0].astype(jnp.float32)
    keep_rate = retention[0]
    length, channels = payload_elements.shape
    short_lag = length // 4
    (local_last,) = drift(keep_rate, payload_elements, jnp.zeros((1, channels), jnp.float32), False)
    factor_last = jnp.prod(keep_rate, axis=0)
    state = jnp.stack([factor_last, local_last[0]])
    both_full, removed = gather_weight(
        jnp.stack([first_conv, second_conv]), state, lambda level: drift(keep_rate, payload_elements, level[None, :], True)[0]
    )
    first_full, second_full = both_full[0], both_full[1]
    trend_removed = removed.astype(jnp.bfloat16)
    tail_rows = trend_removed[length - short_lag :]
    near_tail = passed_along(tail_rows, TM, 1)
    own_past = jnp.concatenate([near_tail, trend_removed[: length - short_lag]], axis=0)
    opening_layer_input = jnp.concatenate([own_past, trend_removed], axis=1)
    stacked_pre = accumulate_with(
        opening_layer_input, first_full
    )
    stacked_out = (trend_removed.astype(jnp.float32) + gated(stacked_pre)).astype(jnp.bfloat16)
    earlier_out = passed_along(stacked_out, TM, 1)
    closing_layer_input = jnp.concatenate([earlier_out, stacked_out], axis=1)
    second_pre = accumulate_with(
        closing_layer_input, second_full
    )
    top_hidden = (stacked_out.astype(jnp.float32) + gated(second_pre)).astype(jnp.bfloat16)
    incoming_gradient = cotangent[0].astype(jnp.float32)
    second_grad = gate_grad(second_pre, incoming_gradient).astype(jnp.bfloat16)
    second_cols = chip_half(weight_term(closing_layer_input, second_grad))
    closing_backward = back_with(
        second_grad, second_full
    )
    carried_back = passed_along(
        closing_backward[:, :channels].astype(jnp.bfloat16), TM, -1
    ).astype(jnp.float32)
    opening_upstream_gradient = incoming_gradient + closing_backward[:, channels:] + carried_back
    first_grad = gate_grad(stacked_pre, opening_upstream_gradient).astype(jnp.bfloat16)
    first_cols = chip_half(weight_term(opening_layer_input, first_grad))
    grads = reduce_gradient(jnp.stack([first_cols, second_cols]))
    grad_first, grad_second = grads[0], grads[1]
    return (top_hidden[None], grad_first, grad_second)


def solution(mesh):
    tm, fsdp = mesh.shape["tm"], mesh.shape["fsdp"]
    split = mesh.devices.reshape(tm // 2, 2, 4, fsdp // 8, 2)
    sub = Mesh(split, SUB_AXES)
    rows, frames = ("x", "y", "zh"), TM
    in_specs = (
        P(rows, frames, None),
        P(rows, frames, None),
        P(rows, None),
        P(rows, None),
        P(rows, frames, None),
    )
    out_specs = (P(rows, frames, None), P(rows, None), P(rows, None))
    return jax.shard_map(
        on_device, mesh=sub, in_specs=in_specs, out_specs=out_specs, check_vma=False
    )
```

```python
import jax
import jax.numpy as jnp
from jax import lax
from jax.experimental import pallas as pl
from jax.sharding import Mesh, PartitionSpec as P


def passed_along(value, axis, steps):
    count = 16
    leading, last = (max(0, -steps), min(count, count - steps))
    return lax.ppermute(value, axis, [(source, source + steps) for source in range(leading, last)])


TM = ("zl", "c")
SUB_AXES = ("zl", "c", "x", "y", "zh")


def rotated(value, axis, size, steps):
    return lax.ppermute(value, axis, [(i, (i + steps) % size) for i in range(size)])


def farthest_first(size):
    return sorted(range(1, size), key=lambda steps: -min(steps, size - steps))


def gather_over(block, axis, size, dim):
    place = lax.axis_index(axis)
    width = block.shape[dim]
    shape = list(block.shape)
    shape[dim] = width * size
    out = lax.dynamic_update_slice_in_dim(jnp.zeros(shape, block.dtype), block, place * width, dim)
    for steps in farthest_first(size):
        arrived = rotated(block, axis, size, steps)
        out = lax.dynamic_update_slice_in_dim(out, arrived, ((place - steps) % size) * width, dim)
    return out


def scatter_over(total, axis, size, dim):
    place = lax.axis_index(axis)
    width = total.shape[dim] // size
    sent = total.astype(jnp.bfloat16)
    acc = lax.dynamic_slice_in_dim(total, place * width, width, dim).astype(jnp.float32)
    for steps in farthest_first(size):
        piece = lax.dynamic_slice_in_dim(sent, ((place + steps) % size) * width, width, dim)
        acc = acc + rotated(piece, axis, size, steps).astype(jnp.float32)
    return acc


def summed_over(total, axis, size):
    stride = size // 2
    while stride >= 1:
        mine = total.astype(jnp.bfloat16)
        partner = lax.ppermute(mine, axis, [(i, i ^ stride) for i in range(size)])
        total = mine.astype(jnp.float32) + partner.astype(jnp.float32)
        stride //= 2
    return total


def halves(value, dim):
    half = value.shape[dim] // 2
    return lax.slice_in_dim(value, 0, half, axis=dim), lax.slice_in_dim(value, half, 2 * half, axis=dim)


def across_halves(value):
    pairs = [(zl * 2 + zh, (zl ^ 4) * 2 + 1 - zh) for zl in range(8) for zh in range(2)]
    return lax.ppermute(value, ("zl", "zh"), pairs)


def gather_halves(block, dim):
    other = across_halves(block)
    first = lax.axis_index("zh") == 0
    return jnp.concatenate([jnp.where(first, block, other), jnp.where(first, other, block)], axis=dim)


def scatter_halves(total, dim):
    keep, give = halves(total, dim)
    first = lax.axis_index("zh") == 0
    kept = jnp.where(first, keep, give).astype(jnp.float32)
    sent = jnp.where(first, give, keep).astype(jnp.bfloat16)
    return kept + across_halves(sent).astype(jnp.float32)


def crossed_pairs(steps, first):
    pairs = []
    for core in range(2):
        for x in range(4):
            for y in range(4):
                if (core == 0) == first:
                    target = (core, (x + steps) % 4, y)
                else:
                    target = (core, x, (y + steps) % 4)
                pairs.append((core * 16 + x * 4 + y, target[0] * 16 + target[1] * 4 + target[2]))
    return pairs


def crossed_place(first):
    core, x, y = lax.axis_index("c"), lax.axis_index("x"), lax.axis_index("y")
    return jnp.where((core == 0) == first, x, y)


def crossed_gather(block, first, dim):
    place = crossed_place(first)
    width = block.shape[dim]
    shape = list(block.shape)
    shape[dim] = width * 4
    out = lax.dynamic_update_slice_in_dim(jnp.zeros(shape, block.dtype), block, place * width, dim)
    for steps in farthest_first(4):
        arrived = lax.ppermute(block, ("c", "x", "y"), crossed_pairs(steps, first))
        out = lax.dynamic_update_slice_in_dim(out, arrived, ((place - steps) % 4) * width, dim)
    return out


def crossed_scatter(total, first, dim):
    place = crossed_place(first)
    width = total.shape[dim] // 4
    sent = total.astype(jnp.bfloat16)
    acc = lax.dynamic_slice_in_dim(total, place * width, width, dim).astype(jnp.float32)
    for steps in farthest_first(4):
        piece = lax.dynamic_slice_in_dim(sent, ((place + steps) % 4) * width, width, dim)
        arrived = lax.ppermute(piece, ("c", "x", "y"), crossed_pairs(steps, first))
        acc = acc + arrived.astype(jnp.float32)
    return acc


def core_order(blocks):
    swapped = jnp.swapaxes(blocks, 1, 2)
    return jnp.where(lax.axis_index("c") == 0, blocks, swapped)


def gather_weight(shard, state, after):
    core = lax.axis_index("c")
    half = shard.shape[2] // 2
    mine = lax.dynamic_slice_in_dim(shard, core * half, half, 2)
    rows = gather_halves(mine, 1)
    ready = carried_level(state, 16)
    rows, _ = lax.optimization_barrier((rows, state))
    count, block, width = rows.shape
    rows = crossed_gather(rows[:, None], False, 1)
    rows, ready = lax.optimization_barrier((rows, ready))
    rows = core_order(crossed_gather(rows[:, None], True, 1))
    rows, done = lax.optimization_barrier((rows, after(ready)))
    rows = rows.reshape(count, 16 * block, width)
    return gather_over(rows, "c", 2, 2), done


def chip_half(partial):
    return scatter_over(partial.astype(jnp.bfloat16), "c", 2, 1)


def reduce_gradient(cols):
    count, height, width = cols.shape
    blocks = core_order(cols.reshape(count, 4, 4, height // 16, width))
    blocks = crossed_scatter(crossed_scatter(blocks, True, 1), False, 2)
    rows = scatter_halves(blocks.reshape(count, height // 16, width), 1)
    total = summed_over(rows, "zl", 8)
    return gather_over(total, "c", 2, 2)


def drift_body(emit, rate_ref, value_ref, start_ref, *out_refs):
    rows = rate_ref.shape[0]

    def block(b, level):
        base = pl.multiple_of(b * 8, 8)
        rate = rate_ref[pl.ds(base, 8), :]
        value = value_ref[pl.ds(base, 8), :]
        for i in range(8):
            keep = rate[i : i + 1, :]
            level = keep * level + (1.0 - keep) * value[i : i + 1, :]
            if emit:
                out_refs[0][pl.ds(base + i, 1), :] = value[i : i + 1, :] - level
        return level

    out_refs[-1][...] = lax.fori_loop(0, rows // 8, block, start_ref[...])


def drift(rate, value, start, emit):
    rows, channels = rate.shape
    outs = [jax.ShapeDtypeStruct((1, channels), jnp.float32)]
    if emit:
        outs = [jax.ShapeDtypeStruct((rows, channels), jnp.float32)] + outs
    return pl.pallas_call(lambda *refs: drift_body(emit, *refs), out_shape=outs)(rate, value, start)


def spread_over(block, axis, count):
    copies = jnp.broadcast_to(block[None], (count,) + block.shape)
    return lax.all_to_all(copies, axis, 0, 0, tiled=True)


def carried_level(state, size):
    place = lax.axis_index(TM)
    every = spread_over(state, TM, size)
    level = jnp.ones_like(state[0]), jnp.zeros_like(state[1])
    for source in range(size - 1):
        joined = combine_maps(level, (every[source, 0], every[source, 1]))
        level = tuple(jnp.where(source < place, j, l) for j, l in zip(joined, level))
    return level[1]


def combine_maps(earlier, later):
    return (earlier[0] * later[0], later[0] * earlier[1] + later[1])


def gated(pre_values):
    split_at = pre_values.shape[1] // 2
    return jnp.tanh(pre_values[:, :split_at]) * jax.nn.sigmoid(pre_values[:, split_at:])


def gate_grad(pre_values, incoming_gradient):
    split_at = pre_values.shape[1] // 2
    tanh_part = jnp.tanh(pre_values[:, :split_at])
    gate_part = jax.nn.sigmoid(pre_values[:, split_at:])
    return jnp.concatenate(
        [
            incoming_gradient * gate_part * (1.0 - tanh_part * tanh_part),
            incoming_gradient * tanh_part * gate_part * (1.0 - gate_part),
        ],
        axis=1,
    )


def accumulate_with(operand, weights_block):
    return jnp.dot(operand, weights_block, preferred_element_type=jnp.float32)


def back_with(gradients, weights_block):
    return lax.dot_general(
        gradients, weights_block, (((1,), (1,)), ((), ())), preferred_element_type=jnp.float32
    )


def weight_term(operand, gradients):
    return lax.dot_general(
        operand, gradients, (((0,), (0,)), ((), ())), preferred_element_type=jnp.float32
    )


def on_device(frames, retention, first_conv, second_conv, cotangent):
    payload_elements = frames[0].astype(jnp.float32)
    keep_rate = retention[0]
    length, channels = payload_elements.shape
    short_lag = length // 4
    (local_last,) = drift(keep_rate, payload_elements, jnp.zeros((1, channels), jnp.float32), False)
    factor_last = jnp.prod(keep_rate, axis=0)
    state = jnp.stack([factor_last, local_last[0]])
    both_full, removed = gather_weight(
        jnp.stack([first_conv, second_conv]), state, lambda level: drift(keep_rate, payload_elements, level[None, :], True)[0]
    )
    first_full, second_full = both_full[0], both_full[1]
    trend_removed = removed.astype(jnp.bfloat16)
    tail_rows = trend_removed[length - short_lag :]
    near_tail = passed_along(tail_rows, TM, 1)
    own_past = jnp.concatenate([near_tail, trend_removed[: length - short_lag]], axis=0)
    opening_layer_input = jnp.concatenate([own_past, trend_removed], axis=1)
    stacked_pre = accumulate_with(
        opening_layer_input, first_full
    )
    stacked_out = (trend_removed.astype(jnp.float32) + gated(stacked_pre)).astype(jnp.bfloat16)
    earlier_out = passed_along(stacked_out, TM, 1)
    closing_layer_input = jnp.concatenate([earlier_out, stacked_out], axis=1)
    second_pre = accumulate_with(
        closing_layer_input, second_full
    )
    top_hidden = (stacked_out.astype(jnp.float32) + gated(second_pre)).astype(jnp.bfloat16)
    incoming_gradient = cotangent[0].astype(jnp.float32)
    second_grad = gate_grad(second_pre, incoming_gradient).astype(jnp.bfloat16)
    second_cols = chip_half(weight_term(closing_layer_input, second_grad))
    closing_backward = back_with(
        second_grad, second_full
    )
    carried_back = passed_along(
        closing_backward[:, :channels].astype(jnp.bfloat16), TM, -1
    ).astype(jnp.float32)
    opening_upstream_gradient = incoming_gradient + closing_backward[:, channels:] + carried_back
    first_grad = gate_grad(stacked_pre, opening_upstream_gradient).astype(jnp.bfloat16)
    first_cols = chip_half(weight_term(opening_layer_input, first_grad))
    grads = reduce_gradient(jnp.stack([first_cols, second_cols]))
    grad_first, grad_second = grads[0], grads[1]
    return (top_hidden[None], grad_first, grad_second)


def solution(mesh):
    tm, fsdp = mesh.shape["tm"], mesh.shape["fsdp"]
    split = mesh.devices.reshape(tm // 2, 2, 4, fsdp // 8, 2)
    sub = Mesh(split, SUB_AXES)
    rows, frames = ("x", "y", "zh"), TM
    in_specs = (
        P(rows, frames, None),
        P(rows, frames, None),
        P(rows, None),
        P(rows, None),
        P(rows, frames, None),
    )
    out_specs = (P(rows, frames, None), P(rows, None), P(rows, None))
    return jax.shard_map(
        on_device, mesh=sub, in_specs=in_specs, out_specs=out_specs, check_vma=False
    )
```

```python
import jax
import jax.numpy as jnp
from jax import lax
from jax.experimental import pallas as pl
from jax.sharding import Mesh, PartitionSpec as P


def passed_along(value, axis, steps):
    count = 16
    leading, last = (max(0, -steps), min(count, count - steps))
    return lax.ppermute(value, axis, [(source, source + steps) for source in range(leading, last)])


TM = ("zl", "c")
SUB_AXES = ("zl", "c", "x", "y", "zh")


def rotated(value, axis, size, steps):
    return lax.ppermute(value, axis, [(i, (i + steps) % size) for i in range(size)])


def farthest_first(size):
    return sorted(range(1, size), key=lambda steps: -min(steps, size - steps))


def gather_over(block, axis, size, dim):
    place = lax.axis_index(axis)
    width = block.shape[dim]
    shape = list(block.shape)
    shape[dim] = width * size
    out = lax.dynamic_update_slice_in_dim(jnp.zeros(shape, block.dtype), block, place * width, dim)
    for steps in farthest_first(size):
        arrived = rotated(block, axis, size, steps)
        out = lax.dynamic_update_slice_in_dim(out, arrived, ((place - steps) % size) * width, dim)
    return out


def scatter_over(total, axis, size, dim):
    place = lax.axis_index(axis)
    width = total.shape[dim] // size
    sent = total.astype(jnp.bfloat16)
    acc = lax.dynamic_slice_in_dim(total, place * width, width, dim).astype(jnp.float32)
    for steps in farthest_first(size):
        piece = lax.dynamic_slice_in_dim(sent, ((place + steps) % size) * width, width, dim)
        acc = acc + rotated(piece, axis, size, steps).astype(jnp.float32)
    return acc


def summed_over(total, axis, size):
    stride = size // 2
    while stride >= 1:
        mine = total.astype(jnp.bfloat16)
        partner = lax.ppermute(mine, axis, [(i, i ^ stride) for i in range(size)])
        total = mine.astype(jnp.float32) + partner.astype(jnp.float32)
        stride //= 2
    return total


def halves(value, dim):
    half = value.shape[dim] // 2
    return lax.slice_in_dim(value, 0, half, axis=dim), lax.slice_in_dim(value, half, 2 * half, axis=dim)


def across_halves(value):
    pairs = [(zl * 2 + zh, (zl ^ 4) * 2 + 1 - zh) for zl in range(8) for zh in range(2)]
    return lax.ppermute(value, ("zl", "zh"), pairs)


def gather_halves(block, dim):
    other = across_halves(block)
    first = lax.axis_index("zh") == 0
    return jnp.concatenate([jnp.where(first, block, other), jnp.where(first, other, block)], axis=dim)


def scatter_halves(total, dim):
    keep, give = halves(total, dim)
    first = lax.axis_index("zh") == 0
    kept = jnp.where(first, keep, give).astype(jnp.float32)
    sent = jnp.where(first, give, keep).astype(jnp.bfloat16)
    return kept + across_halves(sent).astype(jnp.float32)


def crossed_pairs(steps, first):
    pairs = []
    for core in range(2):
        for x in range(4):
            for y in range(4):
                if (core == 0) == first:
                    target = (core, (x + steps) % 4, y)
                else:
                    target = (core, x, (y + steps) % 4)
                pairs.append((core * 16 + x * 4 + y, target[0] * 16 + target[1] * 4 + target[2]))
    return pairs


def crossed_place(first):
    core, x, y = lax.axis_index("c"), lax.axis_index("x"), lax.axis_index("y")
    return jnp.where((core == 0) == first, x, y)


def crossed_gather(block, first, dim):
    place = crossed_place(first)
    width = block.shape[dim]
    shape = list(block.shape)
    shape[dim] = width * 4
    out = lax.dynamic_update_slice_in_dim(jnp.zeros(shape, block.dtype), block, place * width, dim)
    for steps in farthest_first(4):
        arrived = lax.ppermute(block, ("c", "x", "y"), crossed_pairs(steps, first))
        out = lax.dynamic_update_slice_in_dim(out, arrived, ((place - steps) % 4) * width, dim)
    return out


def crossed_scatter(total, first, dim):
    place = crossed_place(first)
    width = total.shape[dim] // 4
    sent = total.astype(jnp.bfloat16)
    acc = lax.dynamic_slice_in_dim(total, place * width, width, dim).astype(jnp.float32)
    for steps in farthest_first(4):
        piece = lax.dynamic_slice_in_dim(sent, ((place + steps) % 4) * width, width, dim)
        arrived = lax.ppermute(piece, ("c", "x", "y"), crossed_pairs(steps, first))
        acc = acc + arrived.astype(jnp.float32)
    return acc


def core_order(blocks):
    swapped = jnp.swapaxes(blocks, 1, 2)
    return jnp.where(lax.axis_index("c") == 0, blocks, swapped)


def gather_weight(shard, state, after):
    core = lax.axis_index("c")
    half = shard.shape[2] // 2
    mine = lax.dynamic_slice_in_dim(shard, core * half, half, 2)
    rows = gather_halves(mine, 1)
    ready = carried_level(state, 16)
    rows, _ = lax.optimization_barrier((rows, state))
    count, block, width = rows.shape
    rows = crossed_gather(rows[:, None], False, 1)
    rows, ready = lax.optimization_barrier((rows, ready))
    rows = core_order(crossed_gather(rows[:, None], True, 1))
    rows, done = lax.optimization_barrier((rows, after(ready)))
    rows = rows.reshape(count, 16 * block, width)
    return [gather_over(rows[i], "c", 2, 1) for i in range(count)], done


def chip_half(partial):
    return scatter_over(partial.astype(jnp.bfloat16), "c", 2, 1)


def reduce_gradient(cols):
    count, height, width = cols.shape
    blocks = core_order(cols.reshape(count, 4, 4, height // 16, width))
    blocks = crossed_scatter(crossed_scatter(blocks, True, 1), False, 2)
    rows = scatter_halves(blocks.reshape(count, height // 16, width), 1)
    total = summed_over(rows, "zl", 8)
    return gather_over(total, "c", 2, 2)


def drift_body(emit, rate_ref, value_ref, start_ref, *out_refs):
    rows = rate_ref.shape[0]

    def block(b, level):
        base = pl.multiple_of(b * 8, 8)
        rate = rate_ref[pl.ds(base, 8), :]
        value = value_ref[pl.ds(base, 8), :]
        for i in range(8):
            keep = rate[i : i + 1, :]
            level = keep * level + (1.0 - keep) * value[i : i + 1, :]
            if emit:
                out_refs[0][pl.ds(base + i, 1), :] = value[i : i + 1, :] - level
        return level

    out_refs[-1][...] = lax.fori_loop(0, rows // 8, block, start_ref[...])


def drift(rate, value, start, emit):
    rows, channels = rate.shape
    outs = [jax.ShapeDtypeStruct((1, channels), jnp.float32)]
    if emit:
        outs = [jax.ShapeDtypeStruct((rows, channels), jnp.float32)] + outs
    return pl.pallas_call(lambda *refs: drift_body(emit, *refs), out_shape=outs)(rate, value, start)


def spread_over(block, axis, count):
    copies = jnp.broadcast_to(block[None], (count,) + block.shape)
    return lax.all_to_all(copies, axis, 0, 0, tiled=True)


def carried_level(state, size):
    place = lax.axis_index(TM)
    every = spread_over(state, TM, size)
    level = jnp.ones_like(state[0]), jnp.zeros_like(state[1])
    for source in range(size - 1):
        joined = combine_maps(level, (every[source, 0], every[source, 1]))
        level = tuple(jnp.where(source < place, j, l) for j, l in zip(joined, level))
    return level[1]


def combine_maps(earlier, later):
    return (earlier[0] * later[0], later[0] * earlier[1] + later[1])


def gated(pre_values):
    split_at = pre_values.shape[1] // 2
    return jnp.tanh(pre_values[:, :split_at]) * jax.nn.sigmoid(pre_values[:, split_at:])


def gate_grad(pre_values, incoming_gradient):
    split_at = pre_values.shape[1] // 2
    tanh_part = jnp.tanh(pre_values[:, :split_at])
    gate_part = jax.nn.sigmoid(pre_values[:, split_at:])
    return jnp.concatenate(
        [
            incoming_gradient * gate_part * (1.0 - tanh_part * tanh_part),
            incoming_gradient * tanh_part * gate_part * (1.0 - gate_part),
        ],
        axis=1,
    )


def accumulate_with(operand, weights_block):
    return jnp.dot(operand, weights_block, preferred_element_type=jnp.float32)


def back_with(gradients, weights_block):
    return lax.dot_general(
        gradients, weights_block, (((1,), (1,)), ((), ())), preferred_element_type=jnp.float32
    )


def weight_term(operand, gradients):
    return lax.dot_general(
        operand, gradients, (((0,), (0,)), ((), ())), preferred_element_type=jnp.float32
    )


def on_device(frames, retention, first_conv, second_conv, cotangent):
    payload_elements = frames[0].astype(jnp.float32)
    keep_rate = retention[0]
    length, channels = payload_elements.shape
    short_lag = length // 4
    (local_last,) = drift(keep_rate, payload_elements, jnp.zeros((1, channels), jnp.float32), False)
    factor_last = jnp.prod(keep_rate, axis=0)
    state = jnp.stack([factor_last, local_last[0]])
    both_full, removed = gather_weight(
        jnp.stack([first_conv, second_conv]), state, lambda level: drift(keep_rate, payload_elements, level[None, :], True)[0]
    )
    first_full, second_full = both_full[0], both_full[1]
    trend_removed = removed.astype(jnp.bfloat16)
    tail_rows = trend_removed[length - short_lag :]
    near_tail = passed_along(tail_rows, TM, 1)
    own_past = jnp.concatenate([near_tail, trend_removed[: length - short_lag]], axis=0)
    opening_layer_input = jnp.concatenate([own_past, trend_removed], axis=1)
    stacked_pre = accumulate_with(
        opening_layer_input, first_full
    )
    stacked_out = (trend_removed.astype(jnp.float32) + gated(stacked_pre)).astype(jnp.bfloat16)
    earlier_out = passed_along(stacked_out, TM, 1)
    closing_layer_input = jnp.concatenate([earlier_out, stacked_out], axis=1)
    second_pre = accumulate_with(
        closing_layer_input, second_full
    )
    top_hidden = (stacked_out.astype(jnp.float32) + gated(second_pre)).astype(jnp.bfloat16)
    incoming_gradient = cotangent[0].astype(jnp.float32)
    second_grad = gate_grad(second_pre, incoming_gradient).astype(jnp.bfloat16)
    second_cols = chip_half(weight_term(closing_layer_input, second_grad))
    closing_backward = back_with(
        second_grad, second_full
    )
    carried_back = passed_along(
        closing_backward[:, :channels].astype(jnp.bfloat16), TM, -1
    ).astype(jnp.float32)
    opening_upstream_gradient = incoming_gradient + closing_backward[:, channels:] + carried_back
    first_grad = gate_grad(stacked_pre, opening_upstream_gradient).astype(jnp.bfloat16)
    first_cols = chip_half(weight_term(opening_layer_input, first_grad))
    grads = reduce_gradient(jnp.stack([first_cols, second_cols]))
    grad_first, grad_second = grads[0], grads[1]
    return (top_hidden[None], grad_first, grad_second)


def solution(mesh):
    tm, fsdp = mesh.shape["tm"], mesh.shape["fsdp"]
    split = mesh.devices.reshape(tm // 2, 2, 4, fsdp // 8, 2)
    sub = Mesh(split, SUB_AXES)
    rows, frames = ("x", "y", "zh"), TM
    in_specs = (
        P(rows, frames, None),
        P(rows, frames, None),
        P(rows, None),
        P(rows, None),
        P(rows, frames, None),
    )
    out_specs = (P(rows, frames, None), P(rows, None), P(rows, None))
    return jax.shard_map(
        on_device, mesh=sub, in_specs=in_specs, out_specs=out_specs, check_vma=False
    )
```
